256 devices in a mesh: req: 32 (over x, z), kv: 8 (over y, core).
Axes of the slice: x: 4, y: 4, z: 8, core: 2. Of those that a mesh axis runs over, the one named last changes fastest.
Arguments:
- states: bfloat16 [256, 2560], P(('req', 'kv')), may hold values from -6 to 6
- norm_gain: bfloat16 [2560], replicated, may hold values from 0.099609375 to 1.8984375
- w_query: bfloat16 [2560, 2560], P(None, 'kv'), may hold values from -0.125 to 0.125
- key_projection_weight: bfloat16 [2560, 640], P(None, 'kv'), may hold values from -0.125 to 0.125
- value_projection_weight: bfloat16 [2560, 640], P(None, 'kv'), may hold values from -0.125 to 0.125
- cache_keys: bfloat16 [256, 8, 80, 4096], P('req', 'kv')
- value_cache_slots: bfloat16 [256, 8, 80, 4096], P('req', 'kv'), may hold values from -6 to 6
- lengths: int32 [256], P('req'), may hold values from 1 to 16383, as said below
- write_pos: int32 [256], P('req'), may hold values from 0 to 4095, as said below
- dealing: int32 [256], replicated, may hold values from 0 to 255, each once
Outputs:
- context: bfloat16 [256, 2560], P(('req', 'kv'))
The draws below stay inside these ranges and needn't reach their ends.
Inputs may be any that keep to these rules, and one draw needn't show every extreme that they name: `lengths`: largest value is reached by some request in every draw. write_pos equals lengths modulo 4096. `dealing`: A permutation of the requests.
All inputs are finite; a program needn't handle non-finite values.
Results may differ from the reference program's by a relative error of at most 0.022.
The reference program's roundings to bfloat16 on the way count: a program that leaves them out, or rounds other values in their place, can miss the bound.
Values may be sent and summed in bfloat16 or wider, within the bound.
No kernel may reach another device: no remote copies, remote signals or barrier semaphores. Data moves between devices by JAX's collectives and lax.ppermute only.
A program may use at most 64 MiB of HBM per device.

```python
import jax
import jax.numpy as jnp
from jax import lax

MODEL_WIDTH = 2560
QUERY_HEADS = 32
KEY_VALUE_HEADS = 8
HEAD_DIMENSION = 80
WINDOW_SLOTS = 4096
MAXLEN = 16384
REQUEST_COUNT = 256


def length_table(key):
    sub_key = jax.random.fold_in(key, 7)
    key_bucket, key_value, key_longest = jax.random.split(sub_key, 3)
    bucket = jax.random.randint(key_bucket, (REQUEST_COUNT,), 0, 4)
    length_caps = jnp.array([MAXLEN, MAXLEN // 4, WINDOW_SLOTS, 24], jnp.int32)
    bucket_cap = length_caps[bucket]
    drawn = jax.random.randint(key_value, (REQUEST_COUNT,), 0, 2 ** 30) % bucket_cap
    drawn = jnp.maximum(drawn, 1)
    longest = jax.random.randint(key_longest, (), 0, REQUEST_COUNT)
    return jnp.where(jnp.arange(REQUEST_COUNT) == longest, MAXLEN - 1, drawn).astype(jnp.int32)


def draw_lengths(key, part):
    return length_table(key)


def draw_write_pos(key, part):
    return (length_table(key) % WINDOW_SLOTS).astype(jnp.int32)


def draw_cache_keys(key, part):
    complete_shape = (REQUEST_COUNT, KEY_VALUE_HEADS, HEAD_DIMENSION, WINDOW_SLOTS)
    normal_part = jax.random.normal(jax.random.fold_in(key, 11), complete_shape, jnp.float32)
    return (normal_part * 2.5).astype(jnp.bfloat16)


def block_levels(stream_key, dims, cuts, least, top_value):
    factor_of, own = 1.0, jax.random.fold_in(stream_key, 6)
    for axis_at, parts in cuts:
        heights = jnp.exp(jax.random.uniform(jax.random.fold_in(own, axis_at), (parts,), jnp.float32, least / len(cuts), top_value / len(cuts)))
        factor_of = factor_of * jnp.repeat(heights, dims[axis_at] // parts).reshape([-1 if axis == axis_at else 1 for axis in range(len(dims))])
    return factor_of


def normal_values(key, dims, deviation, reach, shards=(), held_as=jnp.bfloat16):
    gain = block_levels(key, dims, shards, -0.22, 0.18) if shards else 1.0
    values = jax.random.normal(key, dims, jnp.float32) * deviation * gain
    return jnp.minimum(jnp.maximum(values, -reach), reach).astype(held_as)


def setup_inputs(seed: int = 0) -> dict:
    splits = jax.random.split(jax.random.key(seed), 11)
    return {
        "states": normal_values(splits[0], (REQUEST_COUNT, MODEL_WIDTH), 1.0, 6.0, ((0, 256),)),
        "norm_gain": jnp.clip(1.0 + 0.18 * jax.random.normal(splits[1], (MODEL_WIDTH,), jnp.float32), 0.099609375, 1.8984375).astype(jnp.bfloat16),
        "w_query": normal_values(splits[2], (MODEL_WIDTH, QUERY_HEADS * HEAD_DIMENSION), MODEL_WIDTH ** -0.5, 0.125, ((1, 8),)),
        "key_projection_weight": normal_values(splits[3], (MODEL_WIDTH, KEY_VALUE_HEADS * HEAD_DIMENSION), MODEL_WIDTH ** -0.5, 0.125, ((1, 8),)),
        "value_projection_weight": normal_values(splits[4], (MODEL_WIDTH, KEY_VALUE_HEADS * HEAD_DIMENSION), MODEL_WIDTH ** -0.5, 0.125, ((1, 8),)),
        "cache_keys": draw_cache_keys(jax.random.fold_in(splits[10], 71), 0),
        "value_cache_slots": normal_values(splits[6], (REQUEST_COUNT, KEY_VALUE_HEADS, HEAD_DIMENSION, WINDOW_SLOTS), 1.0, 6.0, ((0, 32), (1, 8))),
        "lengths": draw_lengths(jax.random.fold_in(splits[10], 71), 0),
        "write_pos": draw_write_pos(jax.random.fold_in(splits[10], 71), 0),
        "dealing": jax.random.permutation(splits[9], REQUEST_COUNT).astype(jnp.int32),
    }


def apply_rotary(tensor, positions):
    half_width = tensor.shape[-1] // 2
    frequency = 10000.0 ** (-(jnp.arange(half_width, dtype=jnp.float32) * 2.0 / tensor.shape[-1]))
    angles = positions.astype(jnp.float32)[:, None] * frequency[None, :]
    cosine = jnp.cos(angles)[:, None, :]
    sine_part = jnp.sin(angles)[:, None, :]
    front_half = tensor[..., :half_width]
    back_half = tensor[..., half_width:]
    return jnp.concatenate([front_half * cosine - back_half * sine_part, back_half * cosine + front_half * sine_part], axis=-1)

def reference(states, norm_gain, w_query, key_projection_weight, value_projection_weight, cache_keys, value_cache_slots, lengths, write_pos, dealing):
    dealt_rows = states[dealing].astype(jnp.float32)
    inv_rms = lax.rsqrt(lax.optimization_barrier(jnp.mean(dealt_rows * dealt_rows, axis=1, keepdims=True)) + 1e-05)
    normalized_input = (dealt_rows * inv_rms * norm_gain.astype(jnp.float32)[None, :]).astype(jnp.bfloat16)
    queries_per_group = QUERY_HEADS // KEY_VALUE_HEADS
    query_vectors = jnp.dot(normalized_input, w_query, preferred_element_type=jnp.float32).reshape(REQUEST_COUNT, QUERY_HEADS, HEAD_DIMENSION)
    fresh_key_rows = jnp.dot(normalized_input, key_projection_weight, preferred_element_type=jnp.float32).reshape(REQUEST_COUNT, KEY_VALUE_HEADS, HEAD_DIMENSION)
    fresh_value_rows = jnp.dot(normalized_input, value_projection_weight, preferred_element_type=jnp.float32).reshape(REQUEST_COUNT, KEY_VALUE_HEADS, HEAD_DIMENSION).astype(jnp.bfloat16)
    query_vectors = apply_rotary(query_vectors, lengths).astype(jnp.bfloat16).reshape(REQUEST_COUNT, KEY_VALUE_HEADS, queries_per_group, HEAD_DIMENSION)
    fresh_key_rows = apply_rotary(fresh_key_rows, lengths).astype(jnp.bfloat16)
    score_scale = 1.0 / HEAD_DIMENSION ** 0.5

    def attend(item_tuple):
        query_one, key_one, value_one, keys_cached, values_cached, length, write_slot = item_tuple
        slot_ids = jnp.arange(WINDOW_SLOTS).astype(jnp.int32)
        at_write = slot_ids == write_slot
        key_rows = jnp.where(at_write[None, None, :], key_one[:, :, None], keys_cached)
        value_rows = jnp.where(at_write[None, None, :], value_one[:, :, None], values_cached)
        scores = jnp.einsum('kgh,khw->kgw', query_one.astype(jnp.float32), key_rows.astype(jnp.float32)) * score_scale
        scores = jnp.where((slot_ids <= length)[None, None, :], scores, -jnp.inf)
        row_max = lax.optimization_barrier(jnp.max(scores, axis=-1, keepdims=True))
        expd = jnp.exp(scores - row_max)
        softmax_weights = (expd / lax.optimization_barrier(jnp.sum(expd, axis=-1, keepdims=True))).astype(jnp.bfloat16)
        mixed = jnp.einsum('kgw,khw->kgh', softmax_weights.astype(jnp.float32), value_rows.astype(jnp.float32))
        return mixed.reshape(QUERY_HEADS * HEAD_DIMENSION).astype(jnp.bfloat16)
    attended = lax.map(attend, (query_vectors, fresh_key_rows, fresh_value_rows, cache_keys, value_cache_slots, lengths, write_pos))
    return jnp.zeros_like(attended).at[dealing].set(attended)
```

```python
import jax
import jax.numpy as jnp
from jax import lax
from jax.sharding import PartitionSpec as P

HEAD_DIMENSION = 80


def apply_rotary(tensor, positions):
    half_width = tensor.shape[-1] // 2
    frequency = 10000.0 ** (-(jnp.arange(half_width, dtype=jnp.float32) * 2.0 / tensor.shape[-1]))
    angles = positions.astype(jnp.float32)[:, None] * frequency[None, :]
    cosine = jnp.cos(angles)[:, None, :]
    sine_part = jnp.sin(angles)[:, None, :]
    front_half = tensor[..., :half_width]
    back_half = tensor[..., half_width:]
    return jnp.concatenate(
        [front_half * cosine - back_half * sine_part, back_half * cosine + front_half * sine_part],
        axis=-1,
    )


def local(
    states,
    norm_gain,
    w_query,
    key_projection_weight,
    value_projection_weight,
    cache_keys,
    value_cache_slots,
    lengths,
    write_pos,
    dealing,
):
    kv_count = lax.axis_size("kv")
    per_device = states.shape[0]
    group_rows = per_device * kv_count
    group_index = lax.axis_index("req")
    kv_index = lax.axis_index("kv")
    req_count = lax.axis_size("req")
    dealt_ids = lax.dynamic_slice_in_dim(dealing, group_index * group_rows, group_rows)
    column_rows = lax.all_gather(states, "req", axis=0, tiled=True)
    column_ids = jnp.arange(req_count, dtype=jnp.int32) * kv_count + kv_index
    pick_in = (dealt_ids[:, None] == column_ids[None, :]).astype(jnp.bfloat16)
    own_part = jnp.dot(pick_in, column_rows, preferred_element_type=jnp.float32).astype(jnp.bfloat16)
    dealt_rows = lax.psum(own_part, "kv")
    wide_rows = dealt_rows.astype(jnp.float32)
    inv_rms = lax.rsqrt(jnp.mean(wide_rows * wide_rows, axis=1, keepdims=True) + 1e-05)
    normalized_input = (wide_rows * inv_rms * norm_gain.astype(jnp.float32)[None, :]).astype(
        jnp.bfloat16
    )
    head_size = HEAD_DIMENSION
    heads_dev = key_projection_weight.shape[1] // head_size
    queries_per_group = w_query.shape[1] // key_projection_weight.shape[1]
    window_size = cache_keys.shape[3]
    query_vectors = jnp.dot(normalized_input, w_query, preferred_element_type=jnp.float32).reshape(
        group_rows, heads_dev * queries_per_group, head_size
    )
    query_vectors = (
        apply_rotary(query_vectors, lengths)
        .astype(jnp.bfloat16)
        .reshape(group_rows, heads_dev, queries_per_group, head_size)
    )
    fresh_key_rows = jnp.dot(
        normalized_input, key_projection_weight, preferred_element_type=jnp.float32
    ).reshape(group_rows, heads_dev, head_size)
    fresh_key_rows = apply_rotary(fresh_key_rows, lengths).astype(jnp.bfloat16)
    fresh_value_rows = (
        jnp.dot(normalized_input, value_projection_weight, preferred_element_type=jnp.float32)
        .astype(jnp.bfloat16)
        .reshape(group_rows, heads_dev, head_size)
    )
    score_scale = 1.0 / head_size**0.5
    scores = (
        jnp.einsum("rkgh,rkhw->rkgw", query_vectors, cache_keys, preferred_element_type=jnp.float32)
        * score_scale
    )
    own_score = (
        jnp.einsum(
            "rkgh,rkh->rkg", query_vectors, fresh_key_rows, preferred_element_type=jnp.float32
        )
        * score_scale
    )
    slot_ids = lax.broadcasted_iota(jnp.int32, (group_rows, 1, 1, window_size), 3)
    at_write = slot_ids == write_pos[:, None, None, None]
    scores = jnp.where(at_write, own_score[..., None], scores)
    scores = jnp.where(slot_ids <= lengths[:, None, None, None], scores, -jnp.inf)
    row_max = jnp.max(scores, axis=-1, keepdims=True)
    expd = jnp.exp(scores - row_max)
    softmax_weights = (expd / jnp.sum(expd, axis=-1, keepdims=True)).astype(jnp.bfloat16)
    stale_weights = jnp.where(at_write, jnp.zeros((), jnp.bfloat16), softmax_weights)
    fresh_weight = jnp.sum(
        jnp.where(at_write, softmax_weights, jnp.zeros((), jnp.bfloat16)).astype(jnp.float32),
        axis=-1,
    )
    mixed = jnp.einsum(
        "rkgw,rkhw->rkgh", stale_weights, value_cache_slots, preferred_element_type=jnp.float32
    )
    mixed = mixed + fresh_weight[..., None] * fresh_value_rows[:, :, None, :].astype(jnp.float32)
    attended = mixed.reshape(group_rows, heads_dev * queries_per_group * head_size).astype(
        jnp.bfloat16
    )
    group_context = lax.all_gather(attended, "kv", axis=1, tiled=True)
    pick_out = (column_ids[:, None] == dealt_ids[None, :]).astype(jnp.bfloat16)
    routed = jnp.dot(pick_out, group_context, preferred_element_type=jnp.float32).astype(
        jnp.bfloat16
    )
    result = lax.psum_scatter(routed, "req", scatter_dimension=0, tiled=True)
    return result


def solution(mesh):
    in_specs = (
        P(("req", "kv"), None),
        P(),
        P(None, "kv"),
        P(None, "kv"),
        P(None, "kv"),
        P("req", "kv", None, None),
        P("req", "kv", None, None),
        P("req"),
        P("req"),
        P(),
    )
    out_specs = P(("req", "kv"), None)
    return jax.shard_map(local, mesh=mesh, in_specs=in_specs, out_specs=out_specs, check_vma=False)
```

```python
import jax
import jax.numpy as jnp
from jax import lax
from jax.sharding import PartitionSpec as P

HEAD_DIMENSION = 80


def apply_rotary(tensor, positions):
    half_width = tensor.shape[-1] // 2
    frequency = 10000.0 ** (-(jnp.arange(half_width, dtype=jnp.float32) * 2.0 / tensor.shape[-1]))
    angles = positions.astype(jnp.float32)[:, None] * frequency[None, :]
    cosine = jnp.cos(angles)[:, None, :]
    sine_part = jnp.sin(angles)[:, None, :]
    front_half = tensor[..., :half_width]
    back_half = tensor[..., half_width:]
    return jnp.concatenate(
        [front_half * cosine - back_half * sine_part, back_half * cosine + front_half * sine_part],
        axis=-1,
    )


def local(
    states,
    norm_gain,
    w_query,
    key_projection_weight,
    value_projection_weight,
    cache_keys,
    value_cache_slots,
    lengths,
    write_pos,
    dealing,
):
    kv_count = lax.axis_size("kv")
    req_count = lax.axis_size("req")
    per_device = states.shape[0]
    group_rows = per_device * kv_count
    group_index = lax.axis_index("req")
    kv_index = lax.axis_index("kv")
    total_rows = dealing.shape[0]
    head_size = HEAD_DIMENSION
    heads_dev = key_projection_weight.shape[1] // head_size
    queries_per_group = w_query.shape[1] // key_projection_weight.shape[1]
    window_size = cache_keys.shape[3]
    query_width = w_query.shape[1]
    key_width = key_projection_weight.shape[1]

    row_block = lax.all_gather(states, "kv", axis=0, tiled=True)
    wide_rows = row_block.astype(jnp.float32)
    inv_rms = lax.rsqrt(jnp.mean(wide_rows * wide_rows, axis=1, keepdims=True) + 1e-05)
    normalized_input = (wide_rows * inv_rms * norm_gain.astype(jnp.float32)[None, :]).astype(
        jnp.bfloat16
    )
    raw_query = jnp.dot(normalized_input, w_query, preferred_element_type=jnp.float32)
    raw_key = jnp.dot(normalized_input, key_projection_weight, preferred_element_type=jnp.float32)
    raw_value = (
        jnp.dot(normalized_input, value_projection_weight, preferred_element_type=jnp.float32)
        .astype(jnp.bfloat16)
        .astype(jnp.float32)
    )
    packed = jnp.concatenate([raw_query, raw_key, raw_value], axis=1)

    inverse = jnp.zeros((total_rows,), jnp.int32).at[dealing].set(
        jnp.arange(total_rows, dtype=jnp.int32)
    )
    local_ids = group_index * group_rows + jnp.arange(group_rows, dtype=jnp.int32)
    dest_group = inverse[local_ids] // group_rows
    to_group = dest_group[None, :, None] == jnp.arange(req_count, dtype=jnp.int32)[:, None, None]
    send_rows = jnp.where(to_group, packed[None], jnp.zeros((), jnp.float32))
    recv_rows = lax.all_to_all(send_rows, "req", 0, 0, tiled=True)
    recv_flat = recv_rows.reshape(req_count * group_rows, packed.shape[1])
    dealt_ids = lax.dynamic_slice_in_dim(dealing, group_index * group_rows, group_rows)
    mine = jnp.take(recv_flat, dealt_ids, axis=0)

    query_vectors = mine[:, :query_width].reshape(group_rows, heads_dev * queries_per_group, head_size)
    query_vectors = (
        apply_rotary(query_vectors, lengths)
        .astype(jnp.bfloat16)
        .reshape(group_rows, heads_dev, queries_per_group, head_size)
    )
    fresh_key_rows = mine[:, query_width : query_width + key_width].reshape(
        group_rows, heads_dev, head_size
    )
    fresh_key_rows = apply_rotary(fresh_key_rows, lengths).astype(jnp.bfloat16)
    fresh_value_rows = (
        mine[:, query_width + key_width :].astype(jnp.bfloat16).reshape(group_rows, heads_dev, head_size)
    )
    score_scale = 1.0 / head_size**0.5
    scores = (
        jnp.einsum("rkgh,rkhw->rkgw", query_vectors, cache_keys, preferred_element_type=jnp.float32)
        * score_scale
    )
    own_score = (
        jnp.einsum(
            "rkgh,rkh->rkg", query_vectors, fresh_key_rows, preferred_element_type=jnp.float32
        )
        * score_scale
    )
    slot_ids = lax.broadcasted_iota(jnp.int32, (group_rows, 1, 1, window_size), 3)
    at_write = slot_ids == write_pos[:, None, None, None]
    scores = jnp.where(at_write, own_score[..., None], scores)
    scores = jnp.where(slot_ids <= lengths[:, None, None, None], scores, -jnp.inf)
    row_max = jnp.max(scores, axis=-1, keepdims=True)
    expd = jnp.exp(scores - row_max)
    softmax_weights = (expd / jnp.sum(expd, axis=-1, keepdims=True)).astype(jnp.bfloat16)
    stale_weights = jnp.where(at_write, jnp.zeros((), jnp.bfloat16), softmax_weights)
    fresh_weight = jnp.sum(
        jnp.where(at_write, softmax_weights, jnp.zeros((), jnp.bfloat16)).astype(jnp.float32),
        axis=-1,
    )
    mixed = jnp.einsum(
        "rkgw,rkhw->rkgh", stale_weights, value_cache_slots, preferred_element_type=jnp.float32
    )
    mixed = mixed + fresh_weight[..., None] * fresh_value_rows[:, :, None, :].astype(jnp.float32)
    attended = mixed.reshape(group_rows, heads_dev * queries_per_group * head_size).astype(
        jnp.bfloat16
    )

    pick_out = (
        jnp.arange(total_rows, dtype=jnp.int32)[:, None] == dealt_ids[None, :]
    ).astype(jnp.bfloat16)
    send_out = jnp.dot(pick_out, attended, preferred_element_type=jnp.float32).astype(jnp.bfloat16)
    recv_out = lax.all_to_all(send_out, ("req", "kv"), 0, 0, tiled=True)
    own_index = (group_index * kv_count + kv_index) * per_device
    own_group = inverse[own_index] // group_rows
    blocks = lax.dynamic_slice_in_dim(recv_out, own_group * kv_count, kv_count)
    return blocks.reshape(per_device, kv_count * attended.shape[1])


def solution(mesh):
    in_specs = (
        P(("req", "kv"), None),
        P(),
        P(None, "kv"),
        P(None, "kv"),
        P(None, "kv"),
        P("req", "kv", None, None),
        P("req", "kv", None, None),
        P("req"),
        P("req"),
        P(),
    )
    out_specs = P(("req", "kv"), None)
    return jax.shard_map(local, mesh=mesh, in_specs=in_specs, out_specs=out_specs, check_vma=False)
```

```python
import jax
import jax.numpy as jnp
from jax import lax
from jax.sharding import PartitionSpec as P

HEAD_DIMENSION = 80


def apply_rotary(tensor, positions):
    half_width = tensor.shape[-1] // 2
    frequency = 10000.0 ** (-(jnp.arange(half_width, dtype=jnp.float32) * 2.0 / tensor.shape[-1]))
    angles = positions.astype(jnp.float32)[:, None] * frequency[None, :]
    cosine = jnp.cos(angles)[:, None, :]
    sine_part = jnp.sin(angles)[:, None, :]
    front_half = tensor[..., :half_width]
    back_half = tensor[..., half_width:]
    return jnp.concatenate(
        [front_half * cosine - back_half * sine_part, back_half * cosine + front_half * sine_part],
        axis=-1,
    )


def local(
    states,
    norm_gain,
    w_query,
    key_projection_weight,
    value_projection_weight,
    cache_keys,
    value_cache_slots,
    lengths,
    write_pos,
    dealing,
):
    kv_count = lax.axis_size("kv")
    req_count = lax.axis_size("req")
    per_device = states.shape[0]
    group_rows = per_device * kv_count
    group_index = lax.axis_index("req")
    kv_index = lax.axis_index("kv")
    total_rows = dealing.shape[0]
    head_size = HEAD_DIMENSION
    heads_dev = key_projection_weight.shape[1] // head_size
    queries_per_group = w_query.shape[1] // key_projection_weight.shape[1]
    window_size = cache_keys.shape[3]
    query_width = w_query.shape[1]
    key_width = key_projection_weight.shape[1]

    row_block = lax.all_to_all(
        jnp.broadcast_to(states[None], (kv_count,) + states.shape), "kv", 0, 0, tiled=True
    ).reshape(group_rows, states.shape[1])
    wide_rows = row_block.astype(jnp.float32)
    inv_rms = lax.rsqrt(jnp.mean(wide_rows * wide_rows, axis=1, keepdims=True) + 1e-05)
    normalized_input = (wide_rows * inv_rms * norm_gain.astype(jnp.float32)[None, :]).astype(
        jnp.bfloat16
    )
    raw_query = jnp.dot(normalized_input, w_query, preferred_element_type=jnp.float32)
    raw_key = jnp.dot(normalized_input, key_projection_weight, preferred_element_type=jnp.float32)
    raw_value = (
        jnp.dot(normalized_input, value_projection_weight, preferred_element_type=jnp.float32)
        .astype(jnp.bfloat16)
        .astype(jnp.float32)
    )
    packed = jnp.concatenate([raw_query, raw_key, raw_value], axis=1)

    places = jnp.arange(total_rows, dtype=jnp.int32)
    local_ids = group_index * group_rows + jnp.arange(group_rows, dtype=jnp.int32)
    dest_group = (
        jnp.sum(jnp.where(dealing[None, :] == local_ids[:, None], places[None, :], 0), axis=1)
        // group_rows
    )
    to_group = dest_group[None, :, None] == jnp.arange(req_count, dtype=jnp.int32)[:, None, None]
    send_rows = jnp.where(to_group, packed[None], jnp.zeros((), jnp.float32))
    recv_rows = lax.all_to_all(send_rows, "req", 0, 0, tiled=True)
    recv_flat = recv_rows.reshape(req_count * group_rows, packed.shape[1])
    dealt_ids = lax.dynamic_slice_in_dim(dealing, group_index * group_rows, group_rows)
    mine = jnp.take(recv_flat, dealt_ids, axis=0)

    query_vectors = mine[:, :query_width].reshape(group_rows, heads_dev * queries_per_group, head_size)
    query_vectors = (
        apply_rotary(query_vectors, lengths)
        .astype(jnp.bfloat16)
        .reshape(group_rows, heads_dev, queries_per_group, head_size)
    )
    fresh_key_rows = mine[:, query_width : query_width + key_width].reshape(
        group_rows, heads_dev, head_size
    )
    fresh_key_rows = apply_rotary(fresh_key_rows, lengths).astype(jnp.bfloat16)
    fresh_value_rows = (
        mine[:, query_width + key_width :].astype(jnp.bfloat16).reshape(group_rows, heads_dev, head_size)
    )
    score_scale = 1.0 / head_size**0.5
    scores = (
        jnp.einsum("rkgh,rkhw->rkgw", query_vectors, cache_keys, preferred_element_type=jnp.float32)
        * score_scale
    )
    own_score = (
        jnp.einsum(
            "rkgh,rkh->rkg", query_vectors, fresh_key_rows, preferred_element_type=jnp.float32
        )
        * score_scale
    )
    slot_ids = lax.broadcasted_iota(jnp.int32, (group_rows, 1, 1, window_size), 3)
    at_write = slot_ids == write_pos[:, None, None, None]
    scores = jnp.where(at_write, own_score[..., None], scores)
    scores = jnp.where(slot_ids <= lengths[:, None, None, None], scores, -jnp.inf)
    row_max = jnp.max(scores, axis=-1, keepdims=True)
    expd = jnp.exp(scores - row_max)
    softmax_weights = (expd / jnp.sum(expd, axis=-1, keepdims=True)).astype(jnp.bfloat16)
    stale_weights = jnp.where(at_write, jnp.zeros((), jnp.bfloat16), softmax_weights)
    fresh_weight = jnp.sum(
        jnp.where(at_write, softmax_weights, jnp.zeros((), jnp.bfloat16)).astype(jnp.float32),
        axis=-1,
    )
    mixed = jnp.einsum(
        "rkgw,rkhw->rkgh", stale_weights, value_cache_slots, preferred_element_type=jnp.float32
    )
    mixed = mixed + fresh_weight[..., None] * fresh_value_rows[:, :, None, :].astype(jnp.float32)
    attended = mixed.reshape(group_rows, heads_dev * queries_per_group * head_size).astype(
        jnp.bfloat16
    )

    pick_out = (
        jnp.arange(total_rows, dtype=jnp.int32)[:, None] == dealt_ids[None, :]
    ).astype(jnp.bfloat16)
    send_out = jnp.dot(pick_out, attended, preferred_element_type=jnp.float32).astype(jnp.bfloat16)
    recv_out = lax.all_to_all(send_out, ("req", "kv"), 0, 0, tiled=True)
    own_index = (group_index * kv_count + kv_index) * per_device
    own_group = jnp.sum(jnp.where(dealing == own_index, places, 0)) // group_rows
    blocks = lax.dynamic_slice_in_dim(recv_out, own_group * kv_count, kv_count)
    return blocks.reshape(per_device, kv_count * attended.shape[1])


def solution(mesh):
    in_specs = (
        P(("req", "kv"), None),
        P(),
        P(None, "kv"),
        P(None, "kv"),
        P(None, "kv"),
        P("req", "kv", None, None),
        P("req", "kv", None, None),
        P("req"),
        P("req"),
        P(),
    )
    out_specs = P(("req", "kv"), None)
    return jax.shard_map(local, mesh=mesh, in_specs=in_specs, out_specs=out_specs, check_vma=False)
```

```python
import jax
import jax.numpy as jnp
from jax import lax
from jax.sharding import Mesh, PartitionSpec as P

HEAD_DIMENSION = 80


def apply_rotary(tensor, positions):
    half_width = tensor.shape[-1] // 2
    frequency = 10000.0 ** (-(jnp.arange(half_width, dtype=jnp.float32) * 2.0 / tensor.shape[-1]))
    angles = positions.astype(jnp.float32)[:, None] * frequency[None, :]
    cosine = jnp.cos(angles)[:, None, :]
    sine_part = jnp.sin(angles)[:, None, :]
    front_half = tensor[..., :half_width]
    back_half = tensor[..., half_width:]
    return jnp.concatenate(
        [front_half * cosine - back_half * sine_part, back_half * cosine + front_half * sine_part],
        axis=-1,
    )


def local(
    states,
    norm_gain,
    w_query,
    key_projection_weight,
    value_projection_weight,
    cache_keys,
    value_cache_slots,
    lengths,
    write_pos,
    dealing,
):
    kv_count = lax.axis_size("kv")
    req_hi = lax.axis_size("req_hi")
    req_lo = lax.axis_size("req_lo")
    req_count = req_hi * req_lo
    per_device = states.shape[0]
    group_rows = per_device * kv_count
    group_index = lax.axis_index("req_hi") * req_lo + lax.axis_index("req_lo")
    kv_index = lax.axis_index("kv")
    total_rows = dealing.shape[0]
    head_size = HEAD_DIMENSION
    heads_dev = key_projection_weight.shape[1] // head_size
    queries_per_group = w_query.shape[1] // key_projection_weight.shape[1]
    window_size = cache_keys.shape[3]
    query_width = w_query.shape[1]
    key_width = key_projection_weight.shape[1]

    row_block = lax.all_to_all(
        jnp.broadcast_to(states[None], (kv_count,) + states.shape), "kv", 0, 0, tiled=True
    ).reshape(group_rows, states.shape[1])
    wide_rows = row_block.astype(jnp.float32)
    inv_rms = lax.rsqrt(jnp.mean(wide_rows * wide_rows, axis=1, keepdims=True) + 1e-05)
    normalized_input = (wide_rows * inv_rms * norm_gain.astype(jnp.float32)[None, :]).astype(
        jnp.bfloat16
    )
    raw_query = jnp.dot(normalized_input, w_query, preferred_element_type=jnp.float32)
    raw_key = jnp.dot(normalized_input, key_projection_weight, preferred_element_type=jnp.float32)
    raw_value = (
        jnp.dot(normalized_input, value_projection_weight, preferred_element_type=jnp.float32)
        .astype(jnp.bfloat16)
        .astype(jnp.float32)
    )
    packed = jnp.concatenate([raw_query, raw_key, raw_value], axis=1)

    places = jnp.arange(total_rows, dtype=jnp.int32)
    local_ids = group_index * group_rows + jnp.arange(group_rows, dtype=jnp.int32)
    dest_group = (
        jnp.sum(jnp.where(dealing[None, :] == local_ids[:, None], places[None, :], 0), axis=1)
        // group_rows
    )
    to_lo = (dest_group % req_lo)[None, :, None] == jnp.arange(req_lo, dtype=jnp.int32)[:, None, None]
    lo_rows = lax.all_to_all(
        jnp.where(to_lo, packed[None], jnp.zeros((), jnp.float32)), "req_lo", 0, 0, tiled=True
    )
    lo_ids = (lax.axis_index("req_hi") * req_lo + jnp.arange(req_lo, dtype=jnp.int32))[
        :, None
    ] * group_rows + jnp.arange(group_rows, dtype=jnp.int32)[None, :]
    lo_groups = (
        jnp.sum(
            jnp.where(dealing[None, None, :] == lo_ids[:, :, None], places[None, None, :], 0),
            axis=2,
        )
        // group_rows
    )
    to_hi = (lo_groups // req_lo)[None, :, :, None] == jnp.arange(req_hi, dtype=jnp.int32)[
        :, None, None, None
    ]
    recv_rows = lax.all_to_all(
        jnp.where(to_hi, lo_rows[None], jnp.zeros((), jnp.float32)), "req_hi", 0, 0, tiled=True
    )
    recv_flat = recv_rows.reshape(req_count * group_rows, packed.shape[1])
    dealt_ids = lax.dynamic_slice_in_dim(dealing, group_index * group_rows, group_rows)
    mine = jnp.take(recv_flat, dealt_ids, axis=0)

    query_vectors = mine[:, :query_width].reshape(group_rows, heads_dev * queries_per_group, head_size)
    query_vectors = (
        apply_rotary(query_vectors, lengths)
        .astype(jnp.bfloat16)
        .reshape(group_rows, heads_dev, queries_per_group, head_size)
    )
    fresh_key_rows = mine[:, query_width : query_width + key_width].reshape(
        group_rows, heads_dev, head_size
    )
    fresh_key_rows = apply_rotary(fresh_key_rows, lengths).astype(jnp.bfloat16)
    fresh_value_rows = (
        mine[:, query_width + key_width :].astype(jnp.bfloat16).reshape(group_rows, heads_dev, head_size)
    )
    score_scale = 1.0 / head_size**0.5
    scores = (
        jnp.einsum("rkgh,rkhw->rkgw", query_vectors, cache_keys, preferred_element_type=jnp.float32)
        * score_scale
    )
    own_score = (
        jnp.einsum(
            "rkgh,rkh->rkg", query_vectors, fresh_key_rows, preferred_element_type=jnp.float32
        )
        * score_scale
    )
    slot_ids = lax.broadcasted_iota(jnp.int32, (group_rows, 1, 1, window_size), 3)
    at_write = slot_ids == write_pos[:, None, None, None]
    scores = jnp.where(at_write, own_score[..., None], scores)
    scores = jnp.where(slot_ids <= lengths[:, None, None, None], scores, -jnp.inf)
    row_max = jnp.max(scores, axis=-1, keepdims=True)
    expd = jnp.exp(scores - row_max)
    softmax_weights = (expd / jnp.sum(expd, axis=-1, keepdims=True)).astype(jnp.bfloat16)
    stale_weights = jnp.where(at_write, jnp.zeros((), jnp.bfloat16), softmax_weights)
    fresh_weight = jnp.sum(
        jnp.where(at_write, softmax_weights, jnp.zeros((), jnp.bfloat16)).astype(jnp.float32),
        axis=-1,
    )
    mixed = jnp.einsum(
        "rkgw,rkhw->rkgh", stale_weights, value_cache_slots, preferred_element_type=jnp.float32
    )
    mixed = mixed + fresh_weight[..., None] * fresh_value_rows[:, :, None, :].astype(jnp.float32)
    attended = mixed.reshape(group_rows, heads_dev * queries_per_group * head_size).astype(
        jnp.bfloat16
    )

    pick_out = (
        jnp.arange(total_rows, dtype=jnp.int32)[:, None] == dealt_ids[None, :]
    ).astype(jnp.bfloat16)
    send_out = jnp.dot(pick_out, attended, preferred_element_type=jnp.float32).astype(jnp.bfloat16)
    recv_out = lax.all_to_all(send_out, ("req_hi", "req_lo", "kv"), 0, 0, tiled=True)
    own_index = (group_index * kv_count + kv_index) * per_device
    own_group = jnp.sum(jnp.where(dealing == own_index, places, 0)) // group_rows
    blocks = lax.dynamic_slice_in_dim(recv_out, own_group * kv_count, kv_count)
    return blocks.reshape(per_device, kv_count * attended.shape[1])


def solution(mesh):
    req_devices = mesh.devices[:, 0]
    outer = len({device.coords[0] for device in req_devices})
    if len(req_devices) % outer:
        outer = 1
    split_mesh = Mesh(
        mesh.devices.reshape(outer, len(req_devices) // outer, mesh.devices.shape[1]),
        ("req_hi", "req_lo", "kv"),
    )
    req = ("req_hi", "req_lo")
    in_specs = (
        P(req + ("kv",), None),
        P(),
        P(None, "kv"),
        P(None, "kv"),
        P(None, "kv"),
        P(req, "kv", None, None),
        P(req, "kv", None, None),
        P(req),
        P(req),
        P(),
    )
    out_specs = P(req + ("kv",), None)
    return jax.shard_map(
        local, mesh=split_mesh, in_specs=in_specs, out_specs=out_specs, check_vma=False
    )
```

```python
import jax
import jax.numpy as jnp
from jax import lax
from jax.sharding import PartitionSpec as P

HEAD_DIMENSION = 80


def apply_rotary(tensor, positions):
    half_width = tensor.shape[-1] // 2
    frequency = 10000.0 ** (-(jnp.arange(half_width, dtype=jnp.float32) * 2.0 / tensor.shape[-1]))
    angles = positions.astype(jnp.float32)[:, None] * frequency[None, :]
    cosine = jnp.cos(angles)[:, None, :]
    sine_part = jnp.sin(angles)[:, None, :]
    front_half = tensor[..., :half_width]
    back_half = tensor[..., half_width:]
    return jnp.concatenate(
        [front_half * cosine - back_half * sine_part, back_half * cosine + front_half * sine_part],
        axis=-1,
    )


def local(
    states,
    norm_gain,
    w_query,
    key_projection_weight,
    value_projection_weight,
    cache_keys,
    value_cache_slots,
    lengths,
    write_pos,
    dealing,
):
    kv_count = lax.axis_size("kv")
    req_count = lax.axis_size("req")
    per_device = states.shape[0]
    group_rows = per_device * kv_count
    group_index = lax.axis_index("req")
    kv_index = lax.axis_index("kv")
    total_rows = dealing.shape[0]
    head_size = HEAD_DIMENSION
    heads_dev = key_projection_weight.shape[1] // head_size
    queries_per_group = w_query.shape[1] // key_projection_weight.shape[1]
    window_size = cache_keys.shape[3]
    query_width = w_query.shape[1]
    key_width = key_projection_weight.shape[1]

    row_block = lax.all_to_all(
        jnp.broadcast_to(states[None], (kv_count,) + states.shape), "kv", 0, 0, tiled=True
    ).reshape(group_rows, states.shape[1])
    wide_rows = row_block.astype(jnp.float32)
    inv_rms = lax.rsqrt(jnp.mean(wide_rows * wide_rows, axis=1, keepdims=True) + 1e-05)
    normalized_input = (wide_rows * inv_rms * norm_gain.astype(jnp.float32)[None, :]).astype(
        jnp.bfloat16
    )
    raw_query = jnp.dot(normalized_input, w_query, preferred_element_type=jnp.float32)
    raw_key = jnp.dot(normalized_input, key_projection_weight, preferred_element_type=jnp.float32)
    raw_value = (
        jnp.dot(normalized_input, value_projection_weight, preferred_element_type=jnp.float32)
        .astype(jnp.bfloat16)
        .astype(jnp.float32)
    )
    packed = jnp.concatenate([raw_query, raw_key, raw_value], axis=1)

    places = jnp.arange(total_rows, dtype=jnp.int32)
    local_ids = group_index * group_rows + jnp.arange(group_rows, dtype=jnp.int32)
    own_index = (group_index * kv_count + kv_index) * per_device
    lookup_ids = jnp.concatenate([local_ids, own_index[None]])
    lookup_groups = (
        jnp.sum(jnp.where(dealing[None, :] == lookup_ids[:, None], places[None, :], 0), axis=1)
        // group_rows
    )
    dest_group = lookup_groups[:group_rows]
    to_group = dest_group[None, :, None] == jnp.arange(req_count, dtype=jnp.int32)[:, None, None]
    send_rows = jnp.where(to_group, packed[None], jnp.zeros((), jnp.float32))
    recv_rows = lax.all_to_all(send_rows, "req", 0, 0, tiled=True)
    recv_flat = recv_rows.reshape(req_count * group_rows, packed.shape[1])
    dealt_ids = lax.dynamic_slice_in_dim(dealing, group_index * group_rows, group_rows)
    mine = jnp.take(recv_flat, dealt_ids, axis=0)

    query_vectors = mine[:, :query_width].reshape(group_rows, heads_dev * queries_per_group, head_size)
    query_vectors = (
        apply_rotary(query_vectors, lengths)
        .astype(jnp.bfloat16)
        .reshape(group_rows, heads_dev, queries_per_group, head_size)
    )
    fresh_key_rows = mine[:, query_width : query_width + key_width].reshape(
        group_rows, heads_dev, head_size
    )
    fresh_key_rows = apply_rotary(fresh_key_rows, lengths).astype(jnp.bfloat16)
    fresh_value_rows = (
        mine[:, query_width + key_width :].astype(jnp.bfloat16).reshape(group_rows, heads_dev, head_size)
    )
    score_scale = 1.0 / head_size**0.5
    scores = (
        jnp.einsum("rkgh,rkhw->rkgw", query_vectors, cache_keys, preferred_element_type=jnp.float32)
        * score_scale
    )
    own_score = (
        jnp.einsum(
            "rkgh,rkh->rkg", query_vectors, fresh_key_rows, preferred_element_type=jnp.float32
        )
        * score_scale
    )
    slot_ids = lax.broadcasted_iota(jnp.int32, (group_rows, 1, 1, window_size), 3)
    at_write = slot_ids == write_pos[:, None, None, None]
    scores = jnp.where(at_write, own_score[..., None], scores)
    scores = jnp.where(slot_ids <= lengths[:, None, None, None], scores, -jnp.inf)
    row_max = jnp.max(scores, axis=-1, keepdims=True)
    expd = jnp.exp(scores - row_max)
    softmax_weights = (expd / jnp.sum(expd, axis=-1, keepdims=True)).astype(jnp.bfloat16)
    stale_weights = jnp.where(at_write, jnp.zeros((), jnp.bfloat16), softmax_weights)
    fresh_weight = jnp.sum(
        jnp.where(at_write, softmax_weights, jnp.zeros((), jnp.bfloat16)).astype(jnp.float32),
        axis=-1,
    )
    mixed = jnp.einsum(
        "rkgw,rkhw->rkgh", stale_weights, value_cache_slots, preferred_element_type=jnp.float32
    )
    mixed = mixed + fresh_weight[..., None] * fresh_value_rows[:, :, None, :].astype(jnp.float32)
    attended = mixed.reshape(group_rows, heads_dev * queries_per_group * head_size).astype(
        jnp.bfloat16
    )

    pick_out = (
        jnp.arange(total_rows, dtype=jnp.int32)[:, None] == dealt_ids[None, :]
    ).astype(jnp.bfloat16)
    send_out = jnp.dot(pick_out, attended, preferred_element_type=jnp.float32).astype(jnp.bfloat16)
    recv_out = lax.all_to_all(send_out, ("req", "kv"), 0, 0, tiled=True)
    own_group = lookup_groups[group_rows]
    blocks = lax.dynamic_slice_in_dim(recv_out, own_group * kv_count, kv_count)
    return blocks.reshape(per_device, kv_count * attended.shape[1])


def solution(mesh):
    in_specs = (
        P(("req", "kv"), None),
        P(),
        P(None, "kv"),
        P(None, "kv"),
        P(None, "kv"),
        P("req", "kv", None, None),
        P("req", "kv", None, None),
        P("req"),
        P("req"),
        P(),
    )
    out_specs = P(("req", "kv"), None)
    return jax.shard_map(local, mesh=mesh, in_specs=in_specs, out_specs=out_specs, check_vma=False)
```

```python
import jax
import jax.numpy as jnp
from jax import lax
from jax.sharding import PartitionSpec as P

HEAD_DIMENSION = 80


def apply_rotary(tensor, positions):
    half_width = tensor.shape[-1] // 2
    frequency = 10000.0 ** (-(jnp.arange(half_width, dtype=jnp.float32) * 2.0 / tensor.shape[-1]))
    angles = positions.astype(jnp.float32)[:, None] * frequency[None, :]
    cosine = jnp.cos(angles)[:, None, :]
    sine_part = jnp.sin(angles)[:, None, :]
    front_half = tensor[..., :half_width]
    back_half = tensor[..., half_width:]
    return jnp.concatenate(
        [front_half * cosine - back_half * sine_part, back_half * cosine + front_half * sine_part],
        axis=-1,
    )


def local(
    states,
    norm_gain,
    w_query,
    key_projection_weight,
    value_projection_weight,
    cache_keys,
    value_cache_slots,
    lengths,
    write_pos,
    dealing,
):
    kv_count = lax.axis_size("kv")
    req_count = lax.axis_size("req")
    per_device = states.shape[0]
    group_rows = per_device * kv_count
    group_index = lax.axis_index("req")
    kv_index = lax.axis_index("kv")
    total_rows = dealing.shape[0]
    head_size = HEAD_DIMENSION
    heads_dev = key_projection_weight.shape[1] // head_size
    queries_per_group = w_query.shape[1] // key_projection_weight.shape[1]
    window_size = cache_keys.shape[3]
    query_width = w_query.shape[1]
    key_width = key_projection_weight.shape[1]

    lane_rows = states.reshape(per_device * states.shape[1] // 128, 128)
    row_block = lax.all_to_all(
        jnp.broadcast_to(lane_rows[None], (kv_count,) + lane_rows.shape), "kv", 0, 0, tiled=True
    ).reshape(group_rows, states.shape[1])
    wide_rows = row_block.astype(jnp.float32)
    inv_rms = lax.rsqrt(jnp.mean(wide_rows * wide_rows, axis=1, keepdims=True) + 1e-05)
    normalized_input = (wide_rows * inv_rms * norm_gain.astype(jnp.float32)[None, :]).astype(
        jnp.bfloat16
    )
    raw_query = jnp.dot(normalized_input, w_query, preferred_element_type=jnp.float32)
    raw_key = jnp.dot(normalized_input, key_projection_weight, preferred_element_type=jnp.float32)
    raw_value = (
        jnp.dot(normalized_input, value_projection_weight, preferred_element_type=jnp.float32)
        .astype(jnp.bfloat16)
        .astype(jnp.float32)
    )
    packed = jnp.concatenate([raw_query, raw_key, raw_value], axis=1)

    places = jnp.arange(total_rows, dtype=jnp.int32)
    local_ids = group_index * group_rows + jnp.arange(group_rows, dtype=jnp.int32)
    own_index = (group_index * kv_count + kv_index) * per_device
    lookup_ids = jnp.concatenate([local_ids, own_index[None]])
    lookup_groups = (
        jnp.sum(jnp.where(dealing[None, :] == lookup_ids[:, None], places[None, :], 0), axis=1)
        // group_rows
    )
    dest_group = lookup_groups[:group_rows]
    to_group = dest_group[None, :, None] == jnp.arange(req_count, dtype=jnp.int32)[:, None, None]
    send_rows = jnp.where(to_group, packed[None], jnp.zeros((), jnp.float32))
    recv_rows = lax.all_to_all(send_rows, "req", 0, 0, tiled=True)
    recv_flat = recv_rows.reshape(req_count * group_rows, packed.shape[1])
    dealt_ids = lax.dynamic_slice_in_dim(dealing, group_index * group_rows, group_rows)
    mine = jnp.take(recv_flat, dealt_ids, axis=0)

    query_vectors = mine[:, :query_width].reshape(group_rows, heads_dev * queries_per_group, head_size)
    query_vectors = (
        apply_rotary(query_vectors, lengths)
        .astype(jnp.bfloat16)
        .reshape(group_rows, heads_dev, queries_per_group, head_size)
    )
    fresh_key_rows = mine[:, query_width : query_width + key_width].reshape(
        group_rows, heads_dev, head_size
    )
    fresh_key_rows = apply_rotary(fresh_key_rows, lengths).astype(jnp.bfloat16)
    fresh_value_rows = (
        mine[:, query_width + key_width :].astype(jnp.bfloat16).reshape(group_rows, heads_dev, head_size)
    )
    score_scale = 1.0 / head_size**0.5
    scores = (
        jnp.einsum("rkgh,rkhw->rkgw", query_vectors, cache_keys, preferred_element_type=jnp.float32)
        * score_scale
    )
    own_score = (
        jnp.einsum(
            "rkgh,rkh->rkg", query_vectors, fresh_key_rows, preferred_element_type=jnp.float32
        )
        * score_scale
    )
    slot_ids = lax.broadcasted_iota(jnp.int32, (group_rows, 1, 1, window_size), 3)
    at_write = slot_ids == write_pos[:, None, None, None]
    scores = jnp.where(at_write, own_score[..., None], scores)
    scores = jnp.where(slot_ids <= lengths[:, None, None, None], scores, -jnp.inf)
    row_max = jnp.max(scores, axis=-1, keepdims=True)
    expd = jnp.exp(scores - row_max)
    softmax_weights = (expd / jnp.sum(expd, axis=-1, keepdims=True)).astype(jnp.bfloat16)
    stale_weights = jnp.where(at_write, jnp.zeros((), jnp.bfloat16), softmax_weights)
    fresh_weight = jnp.sum(
        jnp.where(at_write, softmax_weights, jnp.zeros((), jnp.bfloat16)).astype(jnp.float32),
        axis=-1,
    )
    mixed = jnp.einsum(
        "rkgw,rkhw->rkgh", stale_weights, value_cache_slots, preferred_element_type=jnp.float32
    )
    mixed = mixed + fresh_weight[..., None] * fresh_value_rows[:, :, None, :].astype(jnp.float32)
    attended = mixed.reshape(group_rows, heads_dev * queries_per_group * head_size).astype(
        jnp.bfloat16
    )

    pick_out = (
        jnp.arange(total_rows, dtype=jnp.int32)[:, None] == dealt_ids[None, :]
    ).astype(jnp.bfloat16)
    send_out = jnp.dot(pick_out, attended, preferred_element_type=jnp.float32).astype(jnp.bfloat16)
    recv_out = lax.all_to_all(send_out, ("req", "kv"), 0, 0, tiled=True)
    own_group = lookup_groups[group_rows]
    blocks = lax.dynamic_slice_in_dim(recv_out, own_group * kv_count, kv_count)
    return blocks.reshape(per_device, kv_count * attended.shape[1])


def solution(mesh):
    in_specs = (
        P(("req", "kv"), None),
        P(),
        P(None, "kv"),
        P(None, "kv"),
        P(None, "kv"),
        P("req", "kv", None, None),
        P("req", "kv", None, None),
        P("req"),
        P("req"),
        P(),
    )
    out_specs = P(("req", "kv"), None)
    return jax.shard_map(local, mesh=mesh, in_specs=in_specs, out_specs=out_specs, check_vma=False)
```

```python
import jax
import jax.numpy as jnp
from jax import lax
from jax.sharding import PartitionSpec as P

HEAD_DIMENSION = 80


def apply_rotary(tensor, positions):
    half_width = tensor.shape[-1] // 2
    frequency = 10000.0 ** (-(jnp.arange(half_width, dtype=jnp.float32) * 2.0 / tensor.shape[-1]))
    angles = positions.astype(jnp.float32)[:, None] * frequency[None, :]
    cosine = jnp.cos(angles)[:, None, :]
    sine_part = jnp.sin(angles)[:, None, :]
    front_half = tensor[..., :half_width]
    back_half = tensor[..., half_width:]
    return jnp.concatenate(
        [front_half * cosine - back_half * sine_part, back_half * cosine + front_half * sine_part],
        axis=-1,
    )


def local(
    states,
    norm_gain,
    w_query,
    key_projection_weight,
    value_projection_weight,
    cache_keys,
    value_cache_slots,
    lengths,
    write_pos,
    dealing,
):
    kv_count = lax.axis_size("kv")
    req_count = lax.axis_size("req")
    per_device = states.shape[0]
    group_rows = per_device * kv_count
    group_index = lax.axis_index("req")
    kv_index = lax.axis_index("kv")
    total_rows = dealing.shape[0]
    head_size = HEAD_DIMENSION
    heads_dev = key_projection_weight.shape[1] // head_size
    queries_per_group = w_query.shape[1] // key_projection_weight.shape[1]
    window_size = cache_keys.shape[3]
    query_width = w_query.shape[1]
    key_width = key_projection_weight.shape[1]

    lane_rows = states.reshape(per_device * states.shape[1] // 128, 128)
    row_block = lax.all_to_all(
        jnp.broadcast_to(lane_rows[None], (kv_count,) + lane_rows.shape), "kv", 0, 0, tiled=True
    ).reshape(group_rows, states.shape[1])
    wide_rows = row_block.astype(jnp.float32)
    inv_rms = lax.rsqrt(jnp.mean(wide_rows * wide_rows, axis=1, keepdims=True) + 1e-05)
    normalized_input = (wide_rows * inv_rms * norm_gain.astype(jnp.float32)[None, :]).astype(
        jnp.bfloat16
    )
    raw_query = jnp.dot(normalized_input, w_query, preferred_element_type=jnp.float32)
    raw_key = jnp.dot(normalized_input, key_projection_weight, preferred_element_type=jnp.float32)
    raw_value = (
        jnp.dot(normalized_input, value_projection_weight, preferred_element_type=jnp.float32)
        .astype(jnp.bfloat16)
        .astype(jnp.float32)
    )
    packed = jnp.concatenate([raw_query, raw_key, raw_value], axis=1)

    places = jnp.arange(total_rows, dtype=jnp.int32)
    local_ids = group_index * group_rows + jnp.arange(group_rows, dtype=jnp.int32)
    own_index = (group_index * kv_count + kv_index) * per_device
    lookup_ids = jnp.concatenate([local_ids, own_index[None]])
    lookup_groups = (
        jnp.sum(jnp.where(dealing[None, :] == lookup_ids[:, None], places[None, :], 0), axis=1)
        // group_rows
    )
    dest_group = lookup_groups[:group_rows]
    to_group = dest_group[None, :, None] == jnp.arange(req_count, dtype=jnp.int32)[:, None, None]
    send_rows = jnp.where(to_group, packed[None], jnp.zeros((), jnp.float32))
    recv_rows = lax.all_to_all(send_rows, "req", 0, 0, tiled=True)
    recv_flat = recv_rows.reshape(req_count * group_rows, packed.shape[1])
    dealt_ids = lax.dynamic_slice_in_dim(dealing, group_index * group_rows, group_rows)
    mine = jnp.take(recv_flat, dealt_ids, axis=0)

    query_vectors = mine[:, :query_width].reshape(group_rows, heads_dev * queries_per_group, head_size)
    query_vectors = (
        apply_rotary(query_vectors, lengths)
        .astype(jnp.bfloat16)
        .reshape(group_rows, heads_dev, queries_per_group, head_size)
    )
    fresh_key_rows = mine[:, query_width : query_width + key_width].reshape(
        group_rows, heads_dev, head_size
    )
    fresh_key_rows = apply_rotary(fresh_key_rows, lengths).astype(jnp.bfloat16)
    fresh_value_rows = (
        mine[:, query_width + key_width :].astype(jnp.bfloat16).reshape(group_rows, heads_dev, head_size)
    )
    score_scale = 1.0 / head_size**0.5
    scores = (
        jnp.einsum("rkgh,rkhw->rkgw", query_vectors, cache_keys, preferred_element_type=jnp.float32)
        * score_scale
    )
    own_score = (
        jnp.einsum(
            "rkgh,rkh->rkg", query_vectors, fresh_key_rows, preferred_element_type=jnp.float32
        )
        * score_scale
    )
    slot_ids = lax.broadcasted_iota(jnp.int32, (group_rows, 1, 1, window_size), 3)
    at_write = slot_ids == write_pos[:, None, None, None]
    scores = jnp.where(at_write, own_score[..., None], scores)
    scores = jnp.where(slot_ids <= lengths[:, None, None, None], scores, -jnp.inf)
    row_max = jnp.max(scores, axis=-1, keepdims=True)
    expd = jnp.exp(scores - row_max)
    softmax_weights = (expd / jnp.sum(expd, axis=-1, keepdims=True)).astype(jnp.bfloat16)
    stale_weights = jnp.where(at_write, jnp.zeros((), jnp.bfloat16), softmax_weights)
    fresh_weight = jnp.sum(
        jnp.where(at_write, softmax_weights, jnp.zeros((), jnp.bfloat16)).astype(jnp.float32),
        axis=-1,
    )
    mixed = jnp.einsum(
        "rkgw,rkhw->rkgh", stale_weights, value_cache_slots, preferred_element_type=jnp.float32
    )
    mixed = mixed + fresh_weight[..., None] * fresh_value_rows[:, :, None, :].astype(jnp.float32)
    attended = mixed.reshape(group_rows, heads_dev * queries_per_group * head_size).astype(
        jnp.bfloat16
    )

    inverse = jnp.sum(
        jnp.where(dealing[None, :] == places[:, None], places[None, :], 0), axis=1
    )
    in_group = inverse // group_rows == group_index
    slot_of = jnp.where(in_group, inverse % group_rows, 0)
    block_width = attended.shape[1]
    halves = 2 if block_width % 2 == 0 else 1
    split_blocks = attended.reshape(group_rows, halves, block_width // halves)
    send_out = jnp.where(
        in_group[:, None, None], jnp.take(split_blocks, slot_of, axis=0), jnp.zeros((), jnp.bfloat16)
    )
    recv_out = lax.all_to_all(send_out, ("req", "kv"), 0, 0, tiled=True)
    own_group = lookup_groups[group_rows]
    blocks = lax.dynamic_slice_in_dim(recv_out, own_group * kv_count, kv_count)
    return blocks.reshape(per_device, kv_count * attended.shape[1])


def solution(mesh):
    in_specs = (
        P(("req", "kv"), None),
        P(),
        P(None, "kv"),
        P(None, "kv"),
        P(None, "kv"),
        P("req", "kv", None, None),
        P("req", "kv", None, None),
        P("req"),
        P("req"),
        P(),
    )
    out_specs = P(("req", "kv"), None)
    return jax.shard_map(local, mesh=mesh, in_specs=in_specs, out_specs=out_specs, check_vma=False)
```

```python
import jax
import jax.numpy as jnp
from jax import lax
from jax.sharding import PartitionSpec as P

HEAD_DIMENSION = 80


def apply_rotary(tensor, positions):
    half_width = tensor.shape[-1] // 2
    frequency = 10000.0 ** (-(jnp.arange(half_width, dtype=jnp.float32) * 2.0 / tensor.shape[-1]))
    angles = positions.astype(jnp.float32)[:, None] * frequency[None, :]
    cosine = jnp.cos(angles)[:, None, :]
    sine_part = jnp.sin(angles)[:, None, :]
    front_half = tensor[..., :half_width]
    back_half = tensor[..., half_width:]
    return jnp.concatenate(
        [front_half * cosine - back_half * sine_part, back_half * cosine + front_half * sine_part],
        axis=-1,
    )


def local(
    states,
    norm_gain,
    w_query,
    key_projection_weight,
    value_projection_weight,
    cache_keys,
    value_cache_slots,
    lengths,
    write_pos,
    dealing,
):
    kv_count = lax.axis_size("kv")
    req_count = lax.axis_size("req")
    per_device = states.shape[0]
    group_rows = per_device * kv_count
    group_index = lax.axis_index("req")
    kv_index = lax.axis_index("kv")
    total_rows = dealing.shape[0]
    head_size = HEAD_DIMENSION
    heads_dev = key_projection_weight.shape[1] // head_size
    queries_per_group = w_query.shape[1] // key_projection_weight.shape[1]
    window_size = cache_keys.shape[3]
    query_width = w_query.shape[1]
    key_width = key_projection_weight.shape[1]

    lane_rows = states.reshape(per_device * states.shape[1] // 128, 128)
    row_block = lax.all_to_all(
        jnp.broadcast_to(lane_rows[None], (kv_count,) + lane_rows.shape), "kv", 0, 0, tiled=True
    ).reshape(group_rows, states.shape[1])
    wide_rows = row_block.astype(jnp.float32)
    inv_rms = lax.rsqrt(jnp.mean(wide_rows * wide_rows, axis=1, keepdims=True) + 1e-05)
    normalized_input = (wide_rows * inv_rms * norm_gain.astype(jnp.float32)[None, :]).astype(
        jnp.bfloat16
    )
    raw_query = jnp.dot(normalized_input, w_query, preferred_element_type=jnp.float32)
    raw_key = jnp.dot(normalized_input, key_projection_weight, preferred_element_type=jnp.float32)
    raw_value = (
        jnp.dot(normalized_input, value_projection_weight, preferred_element_type=jnp.float32)
        .astype(jnp.bfloat16)
        .astype(jnp.float32)
    )
    packed = jnp.concatenate([raw_query, raw_key, raw_value], axis=1)

    places = jnp.arange(total_rows, dtype=jnp.int32)
    local_ids = group_index * group_rows + jnp.arange(group_rows, dtype=jnp.int32)
    own_index = (group_index * kv_count + kv_index) * per_device
    lookup_ids = jnp.concatenate([local_ids, own_index[None]])
    lookup_groups = (
        jnp.sum(jnp.where(dealing[None, :] == lookup_ids[:, None], places[None, :], 0), axis=1)
        // group_rows
    )
    dest_group = lookup_groups[:group_rows]
    to_group = dest_group[None, :, None] == jnp.arange(req_count, dtype=jnp.int32)[:, None, None]
    send_rows = jnp.where(to_group, packed[None], jnp.zeros((), jnp.float32))
    recv_rows = lax.all_to_all(send_rows, "req", 0, 0, tiled=True)
    recv_flat = recv_rows.reshape(req_count * group_rows, packed.shape[1])
    dealt_ids = lax.dynamic_slice_in_dim(dealing, group_index * group_rows, group_rows)
    mine = jnp.take(recv_flat, dealt_ids, axis=0)

    query_vectors = mine[:, :query_width].reshape(group_rows, heads_dev * queries_per_group, head_size)
    query_vectors = (
        apply_rotary(query_vectors, lengths)
        .astype(jnp.bfloat16)
        .reshape(group_rows, heads_dev, queries_per_group, head_size)
    )
    fresh_key_rows = mine[:, query_width : query_width + key_width].reshape(
        group_rows, heads_dev, head_size
    )
    fresh_key_rows = apply_rotary(fresh_key_rows, lengths).astype(jnp.bfloat16)
    fresh_value_rows = (
        mine[:, query_width + key_width :].astype(jnp.bfloat16).reshape(group_rows, heads_dev, head_size)
    )
    score_scale = 1.0 / head_size**0.5
    scores = (
        jnp.einsum("rkgh,rkhw->rkgw", query_vectors, cache_keys, preferred_element_type=jnp.float32)
        * score_scale
    )
    own_score = (
        jnp.einsum(
            "rkgh,rkh->rkg", query_vectors, fresh_key_rows, preferred_element_type=jnp.float32
        )
        * score_scale
    )
    slot_ids = lax.broadcasted_iota(jnp.int32, (group_rows, 1, 1, window_size), 3)
    at_write = slot_ids == write_pos[:, None, None, None]
    scores = jnp.where(at_write, own_score[..., None], scores)
    scores = jnp.where(slot_ids <= lengths[:, None, None, None], scores, -jnp.inf)
    row_max = jnp.max(scores, axis=-1, keepdims=True)
    expd = jnp.exp(scores - row_max)
    softmax_weights = (expd / jnp.sum(expd, axis=-1, keepdims=True)).astype(jnp.bfloat16)
    stale_weights = jnp.where(at_write, jnp.zeros((), jnp.bfloat16), softmax_weights)
    fresh_weight = jnp.sum(
        jnp.where(at_write, softmax_weights, jnp.zeros((), jnp.bfloat16)).astype(jnp.float32),
        axis=-1,
    )
    mixed = jnp.einsum(
        "rkgw,rkhw->rkgh", stale_weights, value_cache_slots, preferred_element_type=jnp.float32
    )
    mixed = mixed + fresh_weight[..., None] * fresh_value_rows[:, :, None, :].astype(jnp.float32)
    attended = mixed.reshape(group_rows, heads_dev * queries_per_group * head_size).astype(
        jnp.bfloat16
    )

    inverse = jnp.sum(
        jnp.where(dealing[None, :] == places[:, None], places[None, :], 0), axis=1
    )
    in_group = inverse // group_rows == group_index
    slot_of = jnp.where(in_group, inverse % group_rows, group_rows)
    block_width = attended.shape[1]
    halves = 2 if block_width % 2 == 0 else 1
    split_blocks = jnp.concatenate(
        [attended, jnp.zeros((1, block_width), jnp.bfloat16)], axis=0
    ).reshape(group_rows + 1, halves, block_width // halves)
    send_out = split_blocks.at[slot_of].get(mode="promise_in_bounds")
    recv_out = lax.all_to_all(send_out, ("req", "kv"), 0, 0, tiled=True)
    own_group = lookup_groups[group_rows]
    blocks = lax.dynamic_slice_in_dim(recv_out, own_group * kv_count, kv_count)
    return blocks.reshape(per_device, kv_count * attended.shape[1])


def solution(mesh):
    in_specs = (
        P(("req", "kv"), None),
        P(),
        P(None, "kv"),
        P(None, "kv"),
        P(None, "kv"),
        P("req", "kv", None, None),
        P("req", "kv", None, None),
        P("req"),
        P("req"),
        P(),
    )
    out_specs = P(("req", "kv"), None)
    return jax.shard_map(local, mesh=mesh, in_specs=in_specs, out_specs=out_specs, check_vma=False)
```

```python
import jax
import jax.numpy as jnp
from jax import lax
from jax.sharding import PartitionSpec as P

HEAD_DIMENSION = 80


def apply_rotary(tensor, positions):
    half_width = tensor.shape[-1] // 2
    frequency = 10000.0 ** (-(jnp.arange(half_width, dtype=jnp.float32) * 2.0 / tensor.shape[-1]))
    angles = positions.astype(jnp.float32)[:, None] * frequency[None, :]
    cosine = jnp.cos(angles)[:, None, :]
    sine_part = jnp.sin(angles)[:, None, :]
    front_half = tensor[..., :half_width]
    back_half = tensor[..., half_width:]
    return jnp.concatenate(
        [front_half * cosine - back_half * sine_part, back_half * cosine + front_half * sine_part],
        axis=-1,
    )


def local(
    states,
    norm_gain,
    w_query,
    key_projection_weight,
    value_projection_weight,
    cache_keys,
    value_cache_slots,
    lengths,
    write_pos,
    dealing,
):
    kv_count = lax.axis_size("kv")
    req_count = lax.axis_size("req")
    per_device = states.shape[0]
    group_rows = per_device * kv_count
    group_index = lax.axis_index("req")
    kv_index = lax.axis_index("kv")
    total_rows = dealing.shape[0]
    head_size = HEAD_DIMENSION
    heads_dev = key_projection_weight.shape[1] // head_size
    queries_per_group = w_query.shape[1] // key_projection_weight.shape[1]
    window_size = cache_keys.shape[3]
    query_width = w_query.shape[1]
    key_width = key_projection_weight.shape[1]

    lane_rows = states.astype(jnp.float32).reshape(per_device * states.shape[1] // 128, 128)
    row_block = lax.all_to_all(
        jnp.broadcast_to(lane_rows[None], (kv_count,) + lane_rows.shape), "kv", 0, 0, tiled=True
    ).reshape(group_rows, states.shape[1])
    wide_rows = row_block.astype(jnp.float32)
    inv_rms = lax.rsqrt(jnp.mean(wide_rows * wide_rows, axis=1, keepdims=True) + 1e-05)
    normalized_input = (wide_rows * inv_rms * norm_gain.astype(jnp.float32)[None, :]).astype(
        jnp.bfloat16
    )
    raw_query = jnp.dot(normalized_input, w_query, preferred_element_type=jnp.float32)
    raw_key = jnp.dot(normalized_input, key_projection_weight, preferred_element_type=jnp.float32)
    raw_value = (
        jnp.dot(normalized_input, value_projection_weight, preferred_element_type=jnp.float32)
        .astype(jnp.bfloat16)
        .astype(jnp.float32)
    )
    packed = jnp.concatenate([raw_query, raw_key, raw_value], axis=1)

    places = jnp.arange(total_rows, dtype=jnp.int32)
    local_ids = group_index * group_rows + jnp.arange(group_rows, dtype=jnp.int32)
    own_index = (group_index * kv_count + kv_index) * per_device
    lookup_ids = jnp.concatenate([local_ids, own_index[None]])
    lookup_groups = (
        jnp.sum(jnp.where(dealing[None, :] == lookup_ids[:, None], places[None, :], 0), axis=1)
        // group_rows
    )
    dest_group = lookup_groups[:group_rows]
    to_group = dest_group[None, :, None] == jnp.arange(req_count, dtype=jnp.int32)[:, None, None]
    send_rows = jnp.where(to_group, packed[None], jnp.zeros((), jnp.float32))
    recv_rows = lax.all_to_all(send_rows, "req", 0, 0, tiled=True)
    recv_flat = recv_rows.reshape(req_count * group_rows, packed.shape[1])
    dealt_ids = lax.dynamic_slice_in_dim(dealing, group_index * group_rows, group_rows)
    mine = jnp.take(recv_flat, dealt_ids, axis=0)

    query_vectors = mine[:, :query_width].reshape(group_rows, heads_dev * queries_per_group, head_size)
    query_vectors = (
        apply_rotary(query_vectors, lengths)
        .astype(jnp.bfloat16)
        .reshape(group_rows, heads_dev, queries_per_group, head_size)
    )
    fresh_key_rows = mine[:, query_width : query_width + key_width].reshape(
        group_rows, heads_dev, head_size
    )
    fresh_key_rows = apply_rotary(fresh_key_rows, lengths).astype(jnp.bfloat16)
    fresh_value_rows = (
        mine[:, query_width + key_width :].astype(jnp.bfloat16).reshape(group_rows, heads_dev, head_size)
    )
    score_scale = 1.0 / head_size**0.5
    scores = (
        jnp.einsum("rkgh,rkhw->rkgw", query_vectors, cache_keys, preferred_element_type=jnp.float32)
        * score_scale
    )
    own_score = (
        jnp.einsum(
            "rkgh,rkh->rkg", query_vectors, fresh_key_rows, preferred_element_type=jnp.float32
        )
        * score_scale
    )
    slot_ids = lax.broadcasted_iota(jnp.int32, (group_rows, 1, 1, window_size), 3)
    at_write = slot_ids == write_pos[:, None, None, None]
    scores = jnp.where(at_write, own_score[..., None], scores)
    scores = jnp.where(slot_ids <= lengths[:, None, None, None], scores, -jnp.inf)
    row_max = jnp.max(scores, axis=-1, keepdims=True)
    expd = jnp.exp(scores - row_max)
    softmax_weights = (expd / jnp.sum(expd, axis=-1, keepdims=True)).astype(jnp.bfloat16)
    stale_weights = jnp.where(at_write, jnp.zeros((), jnp.bfloat16), softmax_weights)
    fresh_weight = jnp.sum(
        jnp.where(at_write, softmax_weights, jnp.zeros((), jnp.bfloat16)).astype(jnp.float32),
        axis=-1,
    )
    mixed = jnp.einsum(
        "rkgw,rkhw->rkgh", stale_weights, value_cache_slots, preferred_element_type=jnp.float32
    )
    mixed = mixed + fresh_weight[..., None] * fresh_value_rows[:, :, None, :].astype(jnp.float32)
    attended = mixed.reshape(group_rows, heads_dev * queries_per_group * head_size).astype(
        jnp.bfloat16
    )

    pick_out = (
        jnp.arange(total_rows, dtype=jnp.int32)[:, None] == dealt_ids[None, :]
    ).astype(jnp.bfloat16)
    send_out = jnp.dot(pick_out, attended, preferred_element_type=jnp.float32).astype(jnp.bfloat16)
    recv_out = lax.all_to_all(send_out, ("req", "kv"), 0, 0, tiled=True)
    own_group = lookup_groups[group_rows]
    blocks = lax.dynamic_slice_in_dim(recv_out, own_group * kv_count, kv_count)
    return blocks.reshape(per_device, kv_count * attended.shape[1])


def solution(mesh):
    in_specs = (
        P(("req", "kv"), None),
        P(),
        P(None, "kv"),
        P(None, "kv"),
        P(None, "kv"),
        P("req", "kv", None, None),
        P("req", "kv", None, None),
        P("req"),
        P("req"),
        P(),
    )
    out_specs = P(("req", "kv"), None)
    return jax.shard_map(local, mesh=mesh, in_specs=in_specs, out_specs=out_specs, check_vma=False)
```

```python
import jax
import jax.numpy as jnp
from jax import lax
from jax.experimental import pallas as pl
from jax.experimental.pallas import tpu as pltpu
from jax.sharding import PartitionSpec as P

HEAD_DIMENSION = 80


def apply_rotary(tensor, positions):
    half_width = tensor.shape[-1] // 2
    frequency = 10000.0 ** (-(jnp.arange(half_width, dtype=jnp.float32) * 2.0 / tensor.shape[-1]))
    angles = positions.astype(jnp.float32)[:, None] * frequency[None, :]
    cosine = jnp.cos(angles)[:, None, :]
    sine_part = jnp.sin(angles)[:, None, :]
    front_half = tensor[..., :half_width]
    back_half = tensor[..., half_width:]
    return jnp.concatenate(
        [front_half * cosine - back_half * sine_part, back_half * cosine + front_half * sine_part],
        axis=-1,
    )


def stage_kernel(keys_hbm, values_hbm, keys_out, values_out, copy_sems):
    key_copy = pltpu.make_async_copy(keys_hbm, keys_out, copy_sems.at[0])
    value_copy = pltpu.make_async_copy(values_hbm, values_out, copy_sems.at[1])
    key_copy.start()
    value_copy.start()
    key_copy.wait()
    value_copy.wait()


def stage_cache(cache_keys, value_cache):
    shapes = (
        jax.ShapeDtypeStruct(cache_keys.shape, cache_keys.dtype),
        jax.ShapeDtypeStruct(value_cache.shape, value_cache.dtype),
    )
    return pl.pallas_call(
        stage_kernel,
        out_shape=shapes,
        in_specs=[pl.BlockSpec(memory_space=pl.ANY)] * 2,
        out_specs=[pl.BlockSpec(memory_space=pltpu.VMEM)] * 2,
        scratch_shapes=[pltpu.SemaphoreType.DMA((2,))],
        compiler_params=pltpu.CompilerParams(vmem_limit_bytes=32 * 1024 * 1024),
    )(cache_keys, value_cache)


def local(
    states,
    norm_gain,
    w_query,
    key_projection_weight,
    value_projection_weight,
    cache_keys,
    value_cache_slots,
    lengths,
    write_pos,
    dealing,
):
    kv_count = lax.axis_size("kv")
    req_count = lax.axis_size("req")
    per_device = states.shape[0]
    group_rows = per_device * kv_count
    group_index = lax.axis_index("req")
    kv_index = lax.axis_index("kv")
    total_rows = dealing.shape[0]
    head_size = HEAD_DIMENSION
    heads_dev = key_projection_weight.shape[1] // head_size
    queries_per_group = w_query.shape[1] // key_projection_weight.shape[1]
    window_size = cache_keys.shape[3]
    query_width = w_query.shape[1]
    key_width = key_projection_weight.shape[1]

    lane_rows = states.reshape(per_device * states.shape[1] // 128, 128)
    row_block = lax.all_to_all(
        jnp.broadcast_to(lane_rows[None], (kv_count,) + lane_rows.shape), "kv", 0, 0, tiled=True
    ).reshape(group_rows, states.shape[1])
    wide_rows = row_block.astype(jnp.float32)
    inv_rms = lax.rsqrt(jnp.mean(wide_rows * wide_rows, axis=1, keepdims=True) + 1e-05)
    normalized_input = (wide_rows * inv_rms * norm_gain.astype(jnp.float32)[None, :]).astype(
        jnp.bfloat16
    )
    raw_query = jnp.dot(normalized_input, w_query, preferred_element_type=jnp.float32)
    raw_key = jnp.dot(normalized_input, key_projection_weight, preferred_element_type=jnp.float32)
    raw_value = (
        jnp.dot(normalized_input, value_projection_weight, preferred_element_type=jnp.float32)
        .astype(jnp.bfloat16)
        .astype(jnp.float32)
    )
    packed = jnp.concatenate([raw_query, raw_key, raw_value], axis=1)

    places = jnp.arange(total_rows, dtype=jnp.int32)
    local_ids = group_index * group_rows + jnp.arange(group_rows, dtype=jnp.int32)
    own_index = (group_index * kv_count + kv_index) * per_device
    lookup_ids = jnp.concatenate([local_ids, own_index[None]])
    lookup_groups = (
        jnp.sum(jnp.where(dealing[None, :] == lookup_ids[:, None], places[None, :], 0), axis=1)
        // group_rows
    )
    dest_group = lookup_groups[:group_rows]
    to_group = dest_group[None, :, None] == jnp.arange(req_count, dtype=jnp.int32)[:, None, None]
    send_rows = jnp.where(to_group, packed[None], jnp.zeros((), jnp.float32))
    recv_rows = lax.all_to_all(send_rows, "req", 0, 0, tiled=True)
    recv_flat = recv_rows.reshape(req_count * group_rows, packed.shape[1])
    dealt_ids = lax.dynamic_slice_in_dim(dealing, group_index * group_rows, group_rows)
    mine = jnp.take(recv_flat, dealt_ids, axis=0)

    query_vectors = mine[:, :query_width].reshape(group_rows, heads_dev * queries_per_group, head_size)
    query_vectors = (
        apply_rotary(query_vectors, lengths)
        .astype(jnp.bfloat16)
        .reshape(group_rows, heads_dev, queries_per_group, head_size)
    )
    fresh_key_rows = mine[:, query_width : query_width + key_width].reshape(
        group_rows, heads_dev, head_size
    )
    fresh_key_rows = apply_rotary(fresh_key_rows, lengths).astype(jnp.bfloat16)
    fresh_value_rows = (
        mine[:, query_width + key_width :].astype(jnp.bfloat16).reshape(group_rows, heads_dev, head_size)
    )
    cache_keys, value_cache_slots = stage_cache(cache_keys, value_cache_slots)
    score_scale = 1.0 / head_size**0.5
    scores = (
        jnp.einsum("rkgh,rkhw->rkgw", query_vectors, cache_keys, preferred_element_type=jnp.float32)
        * score_scale
    )
    own_score = (
        jnp.einsum(
            "rkgh,rkh->rkg", query_vectors, fresh_key_rows, preferred_element_type=jnp.float32
        )
        * score_scale
    )
    slot_ids = lax.broadcasted_iota(jnp.int32, (group_rows, 1, 1, window_size), 3)
    at_write = slot_ids == write_pos[:, None, None, None]
    scores = jnp.where(at_write, own_score[..., None], scores)
    scores = jnp.where(slot_ids <= lengths[:, None, None, None], scores, -jnp.inf)
    row_max = jnp.max(scores, axis=-1, keepdims=True)
    expd = jnp.exp(scores - row_max)
    softmax_weights = (expd / jnp.sum(expd, axis=-1, keepdims=True)).astype(jnp.bfloat16)
    stale_weights = jnp.where(at_write, jnp.zeros((), jnp.bfloat16), softmax_weights)
    fresh_weight = jnp.sum(
        jnp.where(at_write, softmax_weights, jnp.zeros((), jnp.bfloat16)).astype(jnp.float32),
        axis=-1,
    )
    mixed = jnp.einsum(
        "rkgw,rkhw->rkgh", stale_weights, value_cache_slots, preferred_element_type=jnp.float32
    )
    mixed = mixed + fresh_weight[..., None] * fresh_value_rows[:, :, None, :].astype(jnp.float32)
    attended = mixed.reshape(group_rows, heads_dev * queries_per_group * head_size).astype(
        jnp.bfloat16
    )

    pick_out = (
        jnp.arange(total_rows, dtype=jnp.int32)[:, None] == dealt_ids[None, :]
    ).astype(jnp.bfloat16)
    send_out = jnp.dot(pick_out, attended, preferred_element_type=jnp.float32).astype(jnp.bfloat16)
    recv_out = lax.all_to_all(send_out, ("req", "kv"), 0, 0, tiled=True)
    own_group = lookup_groups[group_rows]
    blocks = lax.dynamic_slice_in_dim(recv_out, own_group * kv_count, kv_count)
    return blocks.reshape(per_device, kv_count * attended.shape[1])


def solution(mesh):
    in_specs = (
        P(("req", "kv"), None),
        P(),
        P(None, "kv"),
        P(None, "kv"),
        P(None, "kv"),
        P("req", "kv", None, None),
        P("req", "kv", None, None),
        P("req"),
        P("req"),
        P(),
    )
    out_specs = P(("req", "kv"), None)
    return jax.shard_map(local, mesh=mesh, in_specs=in_specs, out_specs=out_specs, check_vma=False)
```

```python
import jax
import jax.numpy as jnp
from jax import lax
from jax.sharding import PartitionSpec as P

HEAD_DIMENSION = 80


def apply_rotary(tensor, positions):
    half_width = tensor.shape[-1] // 2
    frequency = 10000.0 ** (-(jnp.arange(half_width, dtype=jnp.float32) * 2.0 / tensor.shape[-1]))
    angles = positions.astype(jnp.float32)[:, None] * frequency[None, :]
    cosine = jnp.cos(angles)[:, None, :]
    sine_part = jnp.sin(angles)[:, None, :]
    front_half = tensor[..., :half_width]
    back_half = tensor[..., half_width:]
    return jnp.concatenate(
        [front_half * cosine - back_half * sine_part, back_half * cosine + front_half * sine_part],
        axis=-1,
    )


def local(
    states,
    norm_gain,
    w_query,
    key_projection_weight,
    value_projection_weight,
    cache_keys,
    value_cache_slots,
    lengths,
    write_pos,
    dealing,
):
    kv_count = lax.axis_size("kv")
    req_count = lax.axis_size("req")
    per_device = states.shape[0]
    group_rows = per_device * kv_count
    group_index = lax.axis_index("req")
    kv_index = lax.axis_index("kv")
    total_rows = dealing.shape[0]
    head_size = HEAD_DIMENSION
    heads_dev = key_projection_weight.shape[1] // head_size
    queries_per_group = w_query.shape[1] // key_projection_weight.shape[1]
    window_size = cache_keys.shape[3]
    query_width = w_query.shape[1]
    key_width = key_projection_weight.shape[1]

    lane_rows = states.reshape(per_device * states.shape[1] // 128, 128)
    row_block = lax.all_to_all(
        jnp.broadcast_to(lane_rows[None], (kv_count,) + lane_rows.shape), "kv", 0, 0, tiled=True
    ).reshape(group_rows, states.shape[1])
    wide_rows = row_block.astype(jnp.float32)
    inv_rms = lax.rsqrt(jnp.mean(wide_rows * wide_rows, axis=1, keepdims=True) + 1e-05)
    normalized_input = (wide_rows * inv_rms * norm_gain.astype(jnp.float32)[None, :]).astype(
        jnp.bfloat16
    )
    raw_query = jnp.dot(normalized_input, w_query, preferred_element_type=jnp.float32)
    raw_key = jnp.dot(normalized_input, key_projection_weight, preferred_element_type=jnp.float32)
    raw_value = (
        jnp.dot(normalized_input, value_projection_weight, preferred_element_type=jnp.float32)
        .astype(jnp.bfloat16)
        .astype(jnp.float32)
    )
    packed = jnp.concatenate([raw_query, raw_key, raw_value], axis=1)

    places = jnp.arange(total_rows, dtype=jnp.int32)
    local_ids = group_index * group_rows + jnp.arange(group_rows, dtype=jnp.int32)
    own_index = (group_index * kv_count + kv_index) * per_device
    lookup_ids = jnp.concatenate([local_ids, own_index[None]])
    lookup_groups = (
        jnp.sum(jnp.where(dealing[None, :] == lookup_ids[:, None], places[None, :], 0), axis=1)
        // group_rows
    )
    dest_group = lookup_groups[:group_rows]
    to_group = dest_group[None, :, None] == jnp.arange(req_count, dtype=jnp.int32)[:, None, None]
    send_rows = jnp.where(to_group, packed[None], jnp.zeros((), jnp.float32))
    recv_rows = lax.all_to_all(send_rows, "req", 0, 0, tiled=True)
    recv_flat = recv_rows.reshape(req_count * group_rows, packed.shape[1])
    dealt_ids = lax.dynamic_slice_in_dim(dealing, group_index * group_rows, group_rows)
    mine = jnp.take(recv_flat, dealt_ids, axis=0)

    query_vectors = mine[:, :query_width].reshape(group_rows, heads_dev * queries_per_group, head_size)
    query_vectors = (
        apply_rotary(query_vectors, lengths)
        .astype(jnp.bfloat16)
        .reshape(group_rows, heads_dev, queries_per_group, head_size)
    )
    fresh_key_rows = mine[:, query_width : query_width + key_width].reshape(
        group_rows, heads_dev, head_size
    )
    fresh_key_rows = apply_rotary(fresh_key_rows, lengths).astype(jnp.bfloat16)
    fresh_value_rows = (
        mine[:, query_width + key_width :].astype(jnp.bfloat16).reshape(group_rows, heads_dev, head_size)
    )
    score_scale = 1.0 / head_size**0.5
    scores = (
        jnp.einsum("rkhw,rkgh->rkwg", cache_keys, query_vectors, preferred_element_type=jnp.float32)
        * score_scale
    )
    own_score = (
        jnp.einsum(
            "rkgh,rkh->rkg", query_vectors, fresh_key_rows, preferred_element_type=jnp.float32
        )
        * score_scale
    )
    slot_ids = lax.broadcasted_iota(jnp.int32, (group_rows, 1, window_size, 1), 2)
    at_write = slot_ids == write_pos[:, None, None, None]
    scores = jnp.where(at_write, own_score[:, :, None, :], scores)
    scores = jnp.where(slot_ids <= lengths[:, None, None, None], scores, -jnp.inf)
    row_max = jnp.max(scores, axis=2, keepdims=True)
    expd = jnp.exp(scores - row_max)
    softmax_weights = (expd / jnp.sum(expd, axis=2, keepdims=True)).astype(jnp.bfloat16)
    stale_weights = jnp.where(at_write, jnp.zeros((), jnp.bfloat16), softmax_weights)
    fresh_weight = jnp.sum(
        jnp.where(at_write, softmax_weights, jnp.zeros((), jnp.bfloat16)).astype(jnp.float32),
        axis=2,
    )
    mixed = jnp.einsum(
        "rkwg,rkhw->rkgh", stale_weights, value_cache_slots, preferred_element_type=jnp.float32
    )
    mixed = mixed + fresh_weight[..., None] * fresh_value_rows[:, :, None, :].astype(jnp.float32)
    attended = mixed.reshape(group_rows, heads_dev * queries_per_group * head_size).astype(
        jnp.bfloat16
    )

    pick_out = (
        jnp.arange(total_rows, dtype=jnp.int32)[:, None] == dealt_ids[None, :]
    ).astype(jnp.bfloat16)
    send_out = jnp.dot(pick_out, attended, preferred_element_type=jnp.float32).astype(jnp.bfloat16)
    recv_out = lax.all_to_all(send_out, ("req", "kv"), 0, 0, tiled=True)
    own_group = lookup_groups[group_rows]
    blocks = lax.dynamic_slice_in_dim(recv_out, own_group * kv_count, kv_count)
    return blocks.reshape(per_device, kv_count * attended.shape[1])


def solution(mesh):
    in_specs = (
        P(("req", "kv"), None),
        P(),
        P(None, "kv"),
        P(None, "kv"),
        P(None, "kv"),
        P("req", "kv", None, None),
        P("req", "kv", None, None),
        P("req"),
        P("req"),
        P(),
    )
    out_specs = P(("req", "kv"), None)
    return jax.shard_map(local, mesh=mesh, in_specs=in_specs, out_specs=out_specs, check_vma=False)
```

```python
import jax
import jax.numpy as jnp
from jax import lax
from jax.sharding import PartitionSpec as P

HEAD_DIMENSION = 80


def apply_rotary(tensor, positions):
    half_width = tensor.shape[-1] // 2
    frequency = 10000.0 ** (-(jnp.arange(half_width, dtype=jnp.float32) * 2.0 / tensor.shape[-1]))
    angles = positions.astype(jnp.float32)[:, None] * frequency[None, :]
    cosine = jnp.cos(angles)[:, None, :]
    sine_part = jnp.sin(angles)[:, None, :]
    front_half = tensor[..., :half_width]
    back_half = tensor[..., half_width:]
    return jnp.concatenate(
        [front_half * cosine - back_half * sine_part, back_half * cosine + front_half * sine_part],
        axis=-1,
    )


def local(
    states,
    norm_gain,
    w_query,
    key_projection_weight,
    value_projection_weight,
    cache_keys,
    value_cache_slots,
    lengths,
    write_pos,
    dealing,
):
    kv_count = lax.axis_size("kv")
    req_count = lax.axis_size("req")
    per_device = states.shape[0]
    group_rows = per_device * kv_count
    group_index = lax.axis_index("req")
    kv_index = lax.axis_index("kv")
    total_rows = dealing.shape[0]
    head_size = HEAD_DIMENSION
    heads_dev = key_projection_weight.shape[1] // head_size
    queries_per_group = w_query.shape[1] // key_projection_weight.shape[1]
    window_size = cache_keys.shape[3]
    query_width = w_query.shape[1]
    key_width = key_projection_weight.shape[1]

    places = jnp.arange(total_rows, dtype=jnp.int32)
    own_index = (group_index * kv_count + kv_index) * per_device
    own_place = jnp.sum(jnp.where(dealing == own_index, places, 0))
    to_group = (own_place // group_rows) == jnp.arange(req_count, dtype=jnp.int32)
    send_rows = jnp.where(to_group[:, None], states, jnp.zeros((), states.dtype))
    recv_rows = lax.all_to_all(send_rows, "req", 0, 0, tiled=True)
    dealt_ids = lax.dynamic_slice_in_dim(dealing, group_index * group_rows, group_rows)
    held = (dealt_ids % kv_count) == kv_index
    slot_rows = jnp.where(
        held[:, None],
        jnp.take(recv_rows, dealt_ids // kv_count, axis=0, mode="clip"),
        jnp.zeros((), states.dtype),
    )
    shared = lax.all_to_all(
        jnp.broadcast_to(slot_rows[None], (kv_count,) + slot_rows.shape), "kv", 0, 0, tiled=True
    )
    wide_rows = jnp.sum(shared.astype(jnp.float32), axis=0)
    inv_rms = lax.rsqrt(jnp.mean(wide_rows * wide_rows, axis=1, keepdims=True) + 1e-05)
    normalized_input = (wide_rows * inv_rms * norm_gain.astype(jnp.float32)[None, :]).astype(
        jnp.bfloat16
    )
    raw_query = jnp.dot(normalized_input, w_query, preferred_element_type=jnp.float32)
    raw_key = jnp.dot(normalized_input, key_projection_weight, preferred_element_type=jnp.float32)
    raw_value = jnp.dot(
        normalized_input, value_projection_weight, preferred_element_type=jnp.float32
    )
    mine = jnp.concatenate([raw_query, raw_key, raw_value], axis=1)

    query_vectors = mine[:, :query_width].reshape(group_rows, heads_dev * queries_per_group, head_size)
    query_vectors = (
        apply_rotary(query_vectors, lengths)
        .astype(jnp.bfloat16)
        .reshape(group_rows, heads_dev, queries_per_group, head_size)
    )
    fresh_key_rows = mine[:, query_width : query_width + key_width].reshape(
        group_rows, heads_dev, head_size
    )
    fresh_key_rows = apply_rotary(fresh_key_rows, lengths).astype(jnp.bfloat16)
    fresh_value_rows = (
        mine[:, query_width + key_width :].astype(jnp.bfloat16).reshape(group_rows, heads_dev, head_size)
    )
    score_scale = 1.0 / head_size**0.5
    scores = (
        jnp.einsum("rkgh,rkhw->rkgw", query_vectors, cache_keys, preferred_element_type=jnp.float32)
        * score_scale
    )
    own_score = (
        jnp.einsum(
            "rkgh,rkh->rkg", query_vectors, fresh_key_rows, preferred_element_type=jnp.float32
        )
        * score_scale
    )
    slot_ids = lax.broadcasted_iota(jnp.int32, (group_rows, 1, 1, window_size), 3)
    at_write = slot_ids == write_pos[:, None, None, None]
    scores = jnp.where(at_write, own_score[..., None], scores)
    scores = jnp.where(slot_ids <= lengths[:, None, None, None], scores, -jnp.inf)
    row_max = jnp.max(scores, axis=-1, keepdims=True)
    expd = jnp.exp(scores - row_max)
    softmax_weights = (expd / jnp.sum(expd, axis=-1, keepdims=True)).astype(jnp.bfloat16)
    stale_weights = jnp.where(at_write, jnp.zeros((), jnp.bfloat16), softmax_weights)
    fresh_weight = jnp.sum(
        jnp.where(at_write, softmax_weights, jnp.zeros((), jnp.bfloat16)).astype(jnp.float32),
        axis=-1,
    )
    mixed = jnp.einsum(
        "rkgw,rkhw->rkgh", stale_weights, value_cache_slots, preferred_element_type=jnp.float32
    )
    mixed = mixed + fresh_weight[..., None] * fresh_value_rows[:, :, None, :].astype(jnp.float32)
    attended = mixed.reshape(group_rows, heads_dev * queries_per_group * head_size).astype(
        jnp.bfloat16
    )

    pick_out = (
        jnp.arange(total_rows, dtype=jnp.int32)[:, None] == dealt_ids[None, :]
    ).astype(jnp.bfloat16)
    send_out = jnp.dot(pick_out, attended, preferred_element_type=jnp.float32).astype(jnp.bfloat16)
    recv_out = lax.all_to_all(send_out, ("req", "kv"), 0, 0, tiled=True)
    own_group = own_place // group_rows
    blocks = lax.dynamic_slice_in_dim(recv_out, own_group * kv_count, kv_count)
    return blocks.reshape(per_device, kv_count * attended.shape[1])


def solution(mesh):
    in_specs = (
        P(("req", "kv"), None),
        P(),
        P(None, "kv"),
        P(None, "kv"),
        P(None, "kv"),
        P("req", "kv", None, None),
        P("req", "kv", None, None),
        P("req"),
        P("req"),
        P(),
    )
    out_specs = P(("req", "kv"), None)
    return jax.shard_map(local, mesh=mesh, in_specs=in_specs, out_specs=out_specs, check_vma=False)
```

```python
import jax
import jax.numpy as jnp
from jax import lax
from jax.sharding import PartitionSpec as P

HEAD_DIMENSION = 80


def apply_rotary(tensor, positions):
    half_width = tensor.shape[-1] // 2
    frequency = 10000.0 ** (-(jnp.arange(half_width, dtype=jnp.float32) * 2.0 / tensor.shape[-1]))
    angles = positions.astype(jnp.float32)[:, None] * frequency[None, :]
    cosine = jnp.cos(angles)[:, None, :]
    sine_part = jnp.sin(angles)[:, None, :]
    front_half = tensor[..., :half_width]
    back_half = tensor[..., half_width:]
    return jnp.concatenate(
        [front_half * cosine - back_half * sine_part, back_half * cosine + front_half * sine_part],
        axis=-1,
    )


def local(
    states,
    norm_gain,
    w_query,
    key_projection_weight,
    value_projection_weight,
    cache_keys,
    value_cache_slots,
    lengths,
    write_pos,
    dealing,
):
    kv_count = lax.axis_size("kv")
    req_count = lax.axis_size("req")
    per_device = states.shape[0]
    group_rows = per_device * kv_count
    group_index = lax.axis_index("req")
    kv_index = lax.axis_index("kv")
    total_rows = dealing.shape[0]
    head_size = HEAD_DIMENSION
    heads_dev = key_projection_weight.shape[1] // head_size
    queries_per_group = w_query.shape[1] // key_projection_weight.shape[1]
    window_size = cache_keys.shape[3]
    query_width = w_query.shape[1]
    key_width = key_projection_weight.shape[1]

    lane_rows = states.reshape(per_device * states.shape[1] // 128, 128)
    row_block = lax.all_to_all(
        jnp.broadcast_to(lane_rows[None], (kv_count,) + lane_rows.shape), "kv", 0, 0, tiled=True
    ).reshape(group_rows, states.shape[1])
    wide_rows = row_block.astype(jnp.float32)
    inv_rms = lax.rsqrt(jnp.mean(wide_rows * wide_rows, axis=1, keepdims=True) + 1e-05)
    normalized_input = (wide_rows * inv_rms * norm_gain.astype(jnp.float32)[None, :]).astype(
        jnp.bfloat16
    )
    raw_query = jnp.dot(normalized_input, w_query, preferred_element_type=jnp.float32)
    raw_key = jnp.dot(normalized_input, key_projection_weight, preferred_element_type=jnp.float32)
    raw_value = (
        jnp.dot(normalized_input, value_projection_weight, preferred_element_type=jnp.float32)
        .astype(jnp.bfloat16)
        .astype(jnp.float32)
    )
    packed = jnp.concatenate([raw_query, raw_key, raw_value], axis=1)

    places = jnp.arange(total_rows, dtype=jnp.int32)
    local_ids = group_index * group_rows + jnp.arange(group_rows, dtype=jnp.int32)
    own_index = (group_index * kv_count + kv_index) * per_device
    lookup_ids = jnp.concatenate([local_ids, own_index[None]])
    lookup_groups = (
        jnp.sum(jnp.where(dealing[None, :] == lookup_ids[:, None], places[None, :], 0), axis=1)
        // group_rows
    )
    dest_group = lookup_groups[:group_rows]
    to_group = dest_group[None, :, None] == jnp.arange(req_count, dtype=jnp.int32)[:, None, None]
    send_rows = jnp.where(to_group, packed[None], jnp.zeros((), jnp.float32))
    recv_rows = lax.all_to_all(send_rows, "req", 0, 0, tiled=True)
    recv_flat = recv_rows.reshape(req_count * group_rows, packed.shape[1])
    dealt_ids = lax.dynamic_slice_in_dim(dealing, group_index * group_rows, group_rows)
    mine = recv_flat.at[dealt_ids].get(mode="promise_in_bounds")

    query_vectors = mine[:, :query_width].reshape(group_rows, heads_dev * queries_per_group, head_size)
    query_vectors = (
        apply_rotary(query_vectors, lengths)
        .astype(jnp.bfloat16)
        .reshape(group_rows, heads_dev, queries_per_group, head_size)
    )
    fresh_key_rows = mine[:, query_width : query_width + key_width].reshape(
        group_rows, heads_dev, head_size
    )
    fresh_key_rows = apply_rotary(fresh_key_rows, lengths).astype(jnp.bfloat16)
    fresh_value_rows = (
        mine[:, query_width + key_width :].astype(jnp.bfloat16).reshape(group_rows, heads_dev, head_size)
    )
    score_scale = 1.0 / head_size**0.5
    scores = (
        jnp.einsum("rkgh,rkhw->rkgw", query_vectors, cache_keys, preferred_element_type=jnp.float32)
        * score_scale
    )
    own_score = (
        jnp.einsum(
            "rkgh,rkh->rkg", query_vectors, fresh_key_rows, preferred_element_type=jnp.float32
        )
        * score_scale
    )
    slot_ids = lax.broadcasted_iota(jnp.int32, (group_rows, 1, 1, window_size), 3)
    at_write = slot_ids == write_pos[:, None, None, None]
    scores = jnp.where(at_write, own_score[..., None], scores)
    scores = jnp.where(slot_ids <= lengths[:, None, None, None], scores, -jnp.inf)
    row_max = jnp.max(scores, axis=-1, keepdims=True)
    expd = jnp.exp(scores - row_max)
    softmax_weights = (expd / jnp.sum(expd, axis=-1, keepdims=True)).astype(jnp.bfloat16)
    stale_weights = jnp.where(at_write, jnp.zeros((), jnp.bfloat16), softmax_weights)
    fresh_weight = jnp.sum(
        jnp.where(at_write, softmax_weights, jnp.zeros((), jnp.bfloat16)).astype(jnp.float32),
        axis=-1,
    )
    mixed = jnp.einsum(
        "rkgw,rkhw->rkgh", stale_weights, value_cache_slots, preferred_element_type=jnp.float32
    )
    mixed = mixed + fresh_weight[..., None] * fresh_value_rows[:, :, None, :].astype(jnp.float32)
    attended = mixed.reshape(group_rows, heads_dev * queries_per_group * head_size).astype(
        jnp.bfloat16
    )

    pick_out = (
        jnp.arange(total_rows, dtype=jnp.int32)[:, None] == dealt_ids[None, :]
    ).astype(jnp.bfloat16)
    send_out = jnp.dot(pick_out, attended, preferred_element_type=jnp.float32).astype(jnp.bfloat16)
    recv_out = lax.all_to_all(send_out, ("req", "kv"), 0, 0, tiled=True)
    own_group = lookup_groups[group_rows]
    blocks = lax.dynamic_slice_in_dim(recv_out, own_group * kv_count, kv_count)
    return blocks.reshape(per_device, kv_count * attended.shape[1])


def solution(mesh):
    in_specs = (
        P(("req", "kv"), None),
        P(),
        P(None, "kv"),
        P(None, "kv"),
        P(None, "kv"),
        P("req", "kv", None, None),
        P("req", "kv", None, None),
        P("req"),
        P("req"),
        P(),
    )
    out_specs = P(("req", "kv"), None)
    return jax.shard_map(local, mesh=mesh, in_specs=in_specs, out_specs=out_specs, check_vma=False)
```

```python
import jax
import jax.numpy as jnp
from jax import lax
from jax.sharding import PartitionSpec as P

HEAD_DIMENSION = 80


def apply_rotary(tensor, positions):
    half_width = tensor.shape[-1] // 2
    frequency = 10000.0 ** (-(jnp.arange(half_width, dtype=jnp.float32) * 2.0 / tensor.shape[-1]))
    angles = positions.astype(jnp.float32)[:, None] * frequency[None, :]
    cosine = jnp.cos(angles)[:, None, :]
    sine_part = jnp.sin(angles)[:, None, :]
    front_half = tensor[..., :half_width]
    back_half = tensor[..., half_width:]
    return jnp.concatenate(
        [front_half * cosine - back_half * sine_part, back_half * cosine + front_half * sine_part],
        axis=-1,
    )


def local(
    states,
    norm_gain,
    w_query,
    key_projection_weight,
    value_projection_weight,
    cache_keys,
    value_cache_slots,
    lengths,
    write_pos,
    dealing,
):
    kv_count = lax.axis_size("kv")
    req_count = lax.axis_size("req")
    per_device = states.shape[0]
    group_rows = per_device * kv_count
    group_index = lax.axis_index("req")
    kv_index = lax.axis_index("kv")
    total_rows = dealing.shape[0]
    head_size = HEAD_DIMENSION
    heads_dev = key_projection_weight.shape[1] // head_size
    queries_per_group = w_query.shape[1] // key_projection_weight.shape[1]
    window_size = cache_keys.shape[3]
    query_width = w_query.shape[1]
    key_width = key_projection_weight.shape[1]

    lane_rows = states.reshape(per_device * states.shape[1] // 128, 128)
    row_block = lax.all_to_all(
        jnp.broadcast_to(lane_rows[None], (kv_count,) + lane_rows.shape), "kv", 0, 0, tiled=True
    ).reshape(group_rows, states.shape[1])
    wide_rows = row_block.astype(jnp.float32)
    inv_rms = lax.rsqrt(jnp.mean(wide_rows * wide_rows, axis=1, keepdims=True) + 1e-05)
    normalized_input = (wide_rows * inv_rms * norm_gain.astype(jnp.float32)[None, :]).astype(
        jnp.bfloat16
    )
    raw_query = jnp.dot(normalized_input, w_query, preferred_element_type=jnp.float32)
    raw_key = jnp.dot(normalized_input, key_projection_weight, preferred_element_type=jnp.float32)
    raw_value = (
        jnp.dot(normalized_input, value_projection_weight, preferred_element_type=jnp.float32)
        .astype(jnp.bfloat16)
        .astype(jnp.float32)
    )
    packed = jnp.concatenate([raw_query, raw_key, raw_value], axis=1)

    places = jnp.arange(total_rows, dtype=jnp.int32)
    local_ids = group_index * group_rows + jnp.arange(group_rows, dtype=jnp.int32)
    own_index = (group_index * kv_count + kv_index) * per_device
    lookup_ids = jnp.concatenate([local_ids, own_index[None]])
    lookup_groups = (
        jnp.sum(jnp.where(dealing[None, :] == lookup_ids[:, None], places[None, :], 0), axis=1)
        // group_rows
    )
    dest_group = lookup_groups[:group_rows]
    to_group = dest_group[None, :, None] == jnp.arange(req_count, dtype=jnp.int32)[:, None, None]
    send_rows = jnp.where(to_group, packed[None], jnp.zeros((), jnp.float32))
    recv_rows = lax.all_to_all(send_rows, "req", 0, 0, tiled=True)
    recv_flat = recv_rows.reshape(req_count * group_rows, packed.shape[1])
    dealt_ids = lax.dynamic_slice_in_dim(dealing, group_index * group_rows, group_rows)
    mine = recv_flat.at[dealt_ids].get(mode="promise_in_bounds")

    query_vectors = mine[:, :query_width].reshape(group_rows, heads_dev * queries_per_group, head_size)
    query_vectors = (
        apply_rotary(query_vectors, lengths)
        .astype(jnp.bfloat16)
        .reshape(group_rows, heads_dev, queries_per_group, head_size)
    )
    fresh_key_rows = mine[:, query_width : query_width + key_width].reshape(
        group_rows, heads_dev, head_size
    )
    fresh_key_rows = apply_rotary(fresh_key_rows, lengths).astype(jnp.bfloat16)
    fresh_value_rows = (
        mine[:, query_width + key_width :].astype(jnp.bfloat16).reshape(group_rows, heads_dev, head_size)
    )
    score_scale = 1.0 / head_size**0.5
    scores = (
        jnp.einsum("rkhw,rkgh->rkwg", cache_keys, query_vectors, preferred_element_type=jnp.float32)
        * score_scale
    )
    own_score = (
        jnp.einsum(
            "rkgh,rkh->rkg", query_vectors, fresh_key_rows, preferred_element_type=jnp.float32
        )
        * score_scale
    )
    slot_ids = lax.broadcasted_iota(jnp.int32, (group_rows, 1, window_size, 1), 2)
    at_write = slot_ids == write_pos[:, None, None, None]
    scores = jnp.where(at_write, own_score[:, :, None, :], scores)
    scores = jnp.where(slot_ids <= lengths[:, None, None, None], scores, -jnp.inf)
    row_max = jnp.max(scores, axis=2, keepdims=True)
    expd = jnp.exp(scores - row_max)
    softmax_weights = (expd / jnp.sum(expd, axis=2, keepdims=True)).astype(jnp.bfloat16)
    stale_weights = jnp.where(at_write, jnp.zeros((), jnp.bfloat16), softmax_weights)
    fresh_weight = jnp.sum(
        jnp.where(at_write, softmax_weights, jnp.zeros((), jnp.bfloat16)).astype(jnp.float32),
        axis=2,
    )
    mixed = jnp.einsum(
        "rkwg,rkhw->rkgh", stale_weights, value_cache_slots, preferred_element_type=jnp.float32
    )
    mixed = mixed + fresh_weight[..., None] * fresh_value_rows[:, :, None, :].astype(jnp.float32)
    attended = mixed.reshape(group_rows, heads_dev * queries_per_group * head_size).astype(
        jnp.bfloat16
    )

    pick_out = (
        jnp.arange(total_rows, dtype=jnp.int32)[:, None] == dealt_ids[None, :]
    ).astype(jnp.bfloat16)
    send_out = jnp.dot(pick_out, attended, preferred_element_type=jnp.float32).astype(jnp.bfloat16)
    recv_out = lax.all_to_all(send_out, ("req", "kv"), 0, 0, tiled=True)
    own_group = lookup_groups[group_rows]
    blocks = lax.dynamic_slice_in_dim(recv_out, own_group * kv_count, kv_count)
    return blocks.reshape(per_device, kv_count * attended.shape[1])


def solution(mesh):
    in_specs = (
        P(("req", "kv"), None),
        P(),
        P(None, "kv"),
        P(None, "kv"),
        P(None, "kv"),
        P("req", "kv", None, None),
        P("req", "kv", None, None),
        P("req"),
        P("req"),
        P(),
    )
    out_specs = P(("req", "kv"), None)
    return jax.shard_map(local, mesh=mesh, in_specs=in_specs, out_specs=out_specs, check_vma=False)
```
